512 devices in a mesh: seq: 128 (over y, z, core), head: 4 (over x).
Axes of the slice: x: 4, y: 8, z: 8, core: 2. Of those that a mesh axis runs over, the one named last changes fastest.
Arguments:
- out_grad: bfloat16 [16384, 4096], P('seq', 'head'), may hold values from -6 to 6
- expert_ids: int32 [16384, 8], P('seq'), may hold values from 0 to 127, all different within a row; in each aligned block of 128 rows (0 to 127, 128 to 255, ...) at most 12 rows name the same one
- top_logits: float32 [16384, 8], P('seq'), may hold values from -10 to 310
- doc_start: int32 [16384], P('seq'), may hold values from 0 to 16383, as said below
- router: bfloat16 [128, 4096], P(None, 'head'), may hold values from -0.09375 to 0.09375
- w_down: bfloat16 [128, 768, 4096], P('seq', None, 'head'), may hold values from -0.21875 to 0.21875
- saved_gu: bfloat16 [128, 2, 768, 1536], P('seq', None, 'head'), may hold values from -6 to 6
- out_weight: bfloat16 [4096, 4096], P('head', 'seq'), may hold values from -0.09375 to 0.09375
- query: bfloat16 [16384, 32, 128], P('seq', 'head'), may hold values from -64 to 64
- key: bfloat16 [16384, 4, 128], P('seq', 'head'), may hold values from -8 to 8
- value: bfloat16 [16384, 4, 128], P('seq', 'head'), may hold values from -6 to 6
Outputs:
- gate_up_grad: bfloat16 [128, 2, 768, 1536], P('seq', None, 'head')
- route_grad: float32 [16384, 8], P('seq')
- query_grad: bfloat16 [16384, 32, 128], P('seq', 'head')
- key_grad: bfloat16 [16384, 4, 128], P('seq', 'head')
- value_grad: bfloat16 [16384, 4, 128], P('seq', 'head')
The draws below stay inside these ranges and needn't reach their ends.
Inputs may be any that keep to these rules, and one draw needn't show every extreme that they name: `expert_ids`: each token names 8 different experts; among the 128 tokens of one index of seq no expert is named by more than 12 tokens. doc_start[t] is the first position of the document that holds t; documents lie end to end, each has at most 896 tokens and one has exactly 896.
All inputs are finite; a program needn't handle non-finite values.
Results may differ from the reference program's by a relative error of at most 0.03.
Values may be sent and summed in bfloat16 or wider, within the bound.
No kernel may reach another device: no remote copies, remote signals or barrier semaphores. Data moves between devices by JAX's collectives and lax.ppermute only.
A program may use at most 128 MiB of HBM per device.

```python
import math
import jax
import jax.numpy as jnp
import numpy as np
from jax import lax

D = 4096
HQ = 32
KV = 4
HD = 128
FFW = 768
TOPK = 8
REACH = 7
TOK_DEV = 128
TOKENS = 16384
EXPERTS = 128
CAP = 12
SLOTS = 1536
MAXDOC = 896
N_SEQ = 128
N_HEAD = 4


def doc_bounds(key):
    long_key = jax.random.fold_in(key, 101)
    short_key = jax.random.fold_in(key, 102)
    kind_key = jax.random.fold_in(key, 103)
    long_len = jax.random.randint(long_key, (TOKENS,), MAXDOC - TOK_DEV // 8, MAXDOC + 1, dtype=jnp.int32)
    short_len = jax.random.randint(short_key, (TOKENS,), 1, MAXDOC + 1, dtype=jnp.int32)
    kind = jax.random.randint(kind_key, (TOKENS,), 0, 4, dtype=jnp.int32)
    lengths = jnp.where(kind < 3, long_len, short_len).astype(jnp.int32)
    positions = jnp.arange(TOKENS, dtype=jnp.int32)
    lengths = jnp.where(positions == 0, MAXDOC, lengths).astype(jnp.int32)
    ends = jnp.cumsum(lengths).astype(jnp.int32)
    starts = ends - lengths
    which = jnp.searchsorted(ends, positions, side='right')
    result = starts[which].astype(jnp.int32)
    return jnp.where(positions == TOKENS - 1, TOKENS - 1, result).astype(jnp.int32)


def draw_doc_start(key, part):
    return doc_bounds(key)


def draw_top_logits(key, part):
    base_key = jax.random.fold_in(key, 201)
    base = jax.random.truncated_normal(base_key, -6.0, 6.0, (TOKENS, TOPK), jnp.float32) * 1.5
    return base


def query_and_key(key):
    key_seed = jax.random.fold_in(key, 11)
    query_seed = jax.random.fold_in(key, 12)
    keys = jax.random.truncated_normal(key_seed, -6.0, 6.0, (TOKENS, KV, HD), jnp.float32)
    queries = jax.random.truncated_normal(query_seed, -6.0, 6.0, (TOKENS, HQ, HD), jnp.float32)
    return (queries, keys)


def draw_query(key, part):
    queries, keys = query_and_key(key)
    return queries.astype(jnp.bfloat16)


def draw_key(key, part):
    queries, keys = query_and_key(key)
    return keys.astype(jnp.bfloat16)


def steps_of(own_key, extent, shards, smallest, high):
    loudness, own = 1.0, jax.random.fold_in(own_key, 6)
    for dim, shards_of in shards:
        heights = jnp.exp(jax.random.uniform(jax.random.fold_in(own, dim), (shards_of,), jnp.float32, smallest / len(shards), high / len(shards)))
        loudness = loudness * jnp.repeat(heights, extent[dim] // shards_of).reshape([-1 if axis == dim else 1 for axis in range(len(extent))])
    return loudness


def deal_out(own_key, own, number, rows, count, top, bound, lean):
    sequence = jax.random.permutation(own_key, count)
    heavy_load, usual = load_shares(count, rows * top, bound, lean, True), load_shares(count, rows * top, bound, lean, False)
    places = jnp.arange(count)

    def named(sizes, rotation):
        used = int((sizes > 0).sum())
        fixed = max(1, used // 4)
        moved = fixed + (places - fixed + rotation * (used - fixed)) % max(1, count - fixed)
        return jnp.zeros((count,), jnp.int32).at[sequence[jnp.where(places < fixed, places, moved)]].set(jnp.asarray(sizes, jnp.int32))

    sizes = jnp.where(number % 4 == 0, named(heavy_load, number // 4), named(usual, number - number // 4 - 1))
    mixed = jax.random.permutation(jax.random.fold_in(own, 3), count)
    source_of, sink = mixed[0:count // 2 * 2:2], mixed[1:count // 2 * 2:2]
    slack = jnp.minimum(sizes[source_of] - 1, bound - sizes[sink]) // 2
    slack = jnp.where((source_of == sequence[0]) | (sink == sequence[0]) | (sizes[sink] == 0), 0, jnp.maximum(slack, 0))
    moved = jax.random.randint(jax.random.fold_in(own, 4), (count // 2,), 0, 1 << 20) % (slack + 1)
    sizes = sizes.at[source_of].add(-moved).at[sink].add(moved)
    members = jnp.searchsorted(jnp.cumsum(sizes), jnp.arange(rows * top), side="right").astype(jnp.int32)
    table = members.reshape(top, rows).T
    table = table[jax.random.permutation(jax.random.fold_in(own, 1), rows)]
    rotation = jax.random.randint(jax.random.fold_in(own, 2), (rows, 1), 0, top)
    return jnp.take_along_axis(table, (jnp.arange(top)[None, :] + rotation) % top, axis=1)


def load_shares(amount, total, bound, slope, full):
    loads = [(1 << 20) // math.isqrt(standing ** slope) + 1 for standing in range(1, amount + 1)]
    largest = bound if full else min(bound, max(-(-total // amount), total * loads[0] // sum(loads)))
    least = 1 if total - largest >= amount - 1 else 0
    holding, rest = [largest] + [least] * (amount - 1), total - largest - least * (amount - 1)
    while rest > 0:
        movable = [i for i in range(1, amount) if holding[i] < largest] or [i for i in range(1, amount) if holding[i] < bound]
        mass, budget = sum([loads[i] for i in movable]), rest
        for i in movable:
            addition = min(bound - holding[i], max(1, budget * loads[i] // mass), rest)
            holding[i] = holding[i] + addition
            rest = rest - addition
    return np.array(holding)


def centred(own_key, dims, scale, reach, pieces=(), kind=jnp.bfloat16):
    drawn = scale * jax.random.normal(own_key, dims, jnp.float32)
    if pieces:
        drawn = drawn * steps_of(own_key, dims, pieces, -0.22, 0.18)
    return jnp.clip(drawn, -reach, reach).astype(kind)


def setup_inputs(seed: int = 0) -> dict:
    arg_keys = jax.random.split(jax.random.key(seed), 12)
    out_grad = centred(arg_keys[0], (TOKENS, D), 1.0, 6.0, ((0, 128), (1, 4)))
    expert_ids_keys = jax.random.split(jax.random.fold_in(arg_keys[1], 1), TOKENS // TOK_DEV)
    expert_ids_turns = jax.random.permutation(jax.random.fold_in(arg_keys[1], 3), TOKENS // TOK_DEV)
    expert_ids = jax.vmap(lambda own, number: deal_out(jax.random.fold_in(arg_keys[1], 2), own, number, TOK_DEV, EXPERTS, TOPK, CAP, 2))(expert_ids_keys, expert_ids_turns).reshape((TOKENS, TOPK))
    top_logits = draw_top_logits(jax.random.fold_in(arg_keys[11], 71), 0)
    doc_start = draw_doc_start(jax.random.fold_in(arg_keys[11], 71), 0)
    router = centred(arg_keys[4], (EXPERTS, D), D ** -0.5, 0.09375, ((1, 4),))
    w_down = centred(arg_keys[5], (EXPERTS, FFW, D), FFW ** -0.5, 0.21875, ((0, 128), (2, 4)))
    saved_gu = centred(arg_keys[6], (EXPERTS, 2, FFW, SLOTS), 1.0, 6.0, ((0, 128), (2, 4)))
    out_weight = centred(arg_keys[7], (HQ * HD, D), (HQ * HD) ** -0.5, 0.09375, ((0, 4), (1, 128)))
    query = draw_query(jax.random.fold_in(arg_keys[11], 71), 0)
    key = draw_key(jax.random.fold_in(arg_keys[11], 71), 0)
    value = centred(arg_keys[10], (TOKENS, KV, HD), 1.0, 6.0, ((0, 128), (1, 4)))
    return dict(out_grad=out_grad, expert_ids=expert_ids, top_logits=top_logits, doc_start=doc_start, router=router, w_down=w_down, saved_gu=saved_gu, out_weight=out_weight, query=query, key=key, value=value)


masked_score = -1.0e30
highest = lax.Precision.HIGHEST


def slot_plan(expert_ids):
    blocked = expert_ids.reshape(N_SEQ, TOK_DEV, TOPK)
    hits = (blocked[:, :, :, None] == jnp.arange(EXPERTS, dtype=jnp.int32)[None, None, None, :]).astype(jnp.int32)
    per_token = jnp.sum(hits, axis=2)
    before = jnp.cumsum(per_token, axis=1) - per_token
    rank = jnp.sum(hits * before[:, :, None, :], axis=3).astype(jnp.int32)
    source = jnp.broadcast_to(jnp.arange(N_SEQ, dtype=jnp.int32)[:, None, None], rank.shape)
    return (source * CAP + rank).reshape(TOKENS, TOPK).astype(jnp.int32)


def attend(queries, upstream, keys_all, values_all, query_pos, key_pos, doc_begin, score_scale):
    qf = queries.astype(jnp.float32)
    gf = upstream.astype(jnp.float32)
    kf = keys_all.astype(jnp.float32)
    vf = values_all.astype(jnp.float32)
    scores = jnp.einsum('tkgd,lkd->kgtl', qf, kf, precision=highest) * score_scale
    valid = (key_pos[None, :] <= query_pos[:, None]) & (key_pos[None, :] >= doc_begin[:, None])
    scores = jnp.where(valid[None, None], scores, masked_score)
    row_max = jnp.max(scores, axis=3, keepdims=True)
    exponent = jnp.exp(scores - row_max)
    probs = exponent / jnp.sum(exponent, axis=3, keepdims=True)
    dprob = jnp.einsum('tkgd,lkd->kgtl', gf, vf, precision=highest)
    row_dot = jnp.sum(probs * dprob, axis=3, keepdims=True)
    probs_b = probs.astype(jnp.bfloat16).astype(jnp.float32)
    dscore = (probs * (dprob - row_dot)).astype(jnp.bfloat16).astype(jnp.float32)
    query_part = jnp.einsum('kgtl,lkd->tkgd', dscore, kf, precision=highest) * score_scale
    key_part = jnp.einsum('kgtl,tkgd->lkd', dscore, qf, precision=highest) * score_scale
    value_part = jnp.einsum('kgtl,tkgd->lkd', probs_b, gf, precision=highest)
    return query_part, key_part, value_part


def reference(out_grad, expert_ids, top_logits, doc_start, router, w_down, saved_gu, out_weight, query, key, value):
    weights = jax.nn.softmax(top_logits, axis=1)
    slots = slot_plan(expert_ids)
    flat_expert = expert_ids.reshape(-1).astype(jnp.int32)
    flat_slot = slots.reshape(-1)
    token_of = jnp.repeat(jnp.arange(TOKENS, dtype=jnp.int32), TOPK)
    table = jnp.full((EXPERTS, SLOTS), TOKENS, jnp.int32).at[flat_expert, flat_slot].set(token_of)
    weight_table = jnp.zeros((EXPERTS, SLOTS), jnp.float32).at[flat_expert, flat_slot].set(weights.reshape(-1))
    weight_table = weight_table.astype(jnp.bfloat16)
    padded_rows = jnp.concatenate([out_grad, jnp.zeros((1, D), out_grad.dtype)], axis=0)
    block = D // N_HEAD

    def expert_step(inputs):
        row_index, slot_weight, weight_e, saved_e = inputs
        rows = padded_rows[row_index]
        raw = jnp.zeros((FFW, SLOTS), jnp.float32)
        for part in range(N_HEAD):
            partial_value = lax.dot_general(weight_e[:, part * block:(part + 1) * block], rows[:, part * block:(part + 1) * block], (((1,), (1,)), ((), ())), preferred_element_type=jnp.float32)
            partial_value = lax.optimization_barrier(partial_value.astype(jnp.bfloat16))
            raw = raw + partial_value.astype(jnp.float32)
        gate = saved_e[0].astype(jnp.float32)
        up = saved_e[1].astype(jnp.float32)
        sig = jax.nn.sigmoid(gate)
        act = gate * sig
        hidden = act * up
        slot_grad = jnp.sum(hidden * raw, axis=0)
        scaled = raw * slot_weight.astype(jnp.float32)[None, :]
        grads = jnp.stack([scaled * up * sig * (1.0 + gate * (1.0 - sig)), scaled * act])
        return grads.astype(jnp.bfloat16), slot_grad

    gate_up_grad, slot_grad = lax.map(expert_step, (table, weight_table, w_down, saved_gu))
    route_grad = slot_grad[flat_expert, flat_slot].reshape(TOKENS, TOPK)
    logit_grad = weights * (route_grad - jnp.sum(weights * route_grad, axis=1, keepdims=True))
    one_hot = jax.nn.one_hot(expert_ids, EXPERTS, dtype=jnp.float32)
    dense = jnp.einsum('tk,tke->te', logit_grad, one_hot, precision=highest)
    router_term = jnp.dot(dense, router.astype(jnp.float32), precision=highest)
    input_grad = (out_grad.astype(jnp.float32) + router_term).astype(jnp.bfloat16)
    attn_grad = jnp.dot(input_grad, out_weight.T, preferred_element_type=jnp.float32).astype(jnp.bfloat16)
    attn_grad = attn_grad.reshape(TOKENS, HQ, HD)

    group = HQ // KV
    score_scale = HD ** -0.5
    span = (REACH + 1) * TOK_DEV
    lead = REACH * TOK_DEV
    pad_keys = jnp.concatenate([jnp.zeros((lead, KV, HD), key.dtype), key], axis=0)
    pad_values = jnp.concatenate([jnp.zeros((lead, KV, HD), value.dtype), value], axis=0)

    def block_step(carry, index):
        start = (index * TOK_DEV).astype(jnp.int32)
        queries = lax.dynamic_slice_in_dim(query, start, TOK_DEV, 0).reshape(TOK_DEV, KV, group, HD)
        upstream = lax.dynamic_slice_in_dim(attn_grad, start, TOK_DEV, 0).reshape(TOK_DEV, KV, group, HD)
        keys_all = lax.dynamic_slice_in_dim(pad_keys, start, span, 0)
        values_all = lax.dynamic_slice_in_dim(pad_values, start, span, 0)
        doc_begin = lax.dynamic_slice_in_dim(doc_start, start, TOK_DEV, 0)
        query_pos = start + jnp.arange(TOK_DEV, dtype=jnp.int32)
        key_pos = start - lead + jnp.arange(span, dtype=jnp.int32)
        query_part, key_part, value_part = attend(queries, upstream, keys_all, values_all, query_pos, key_pos, doc_begin, score_scale)
        old = lax.dynamic_slice_in_dim(carry, start, span, 1)
        carry = lax.dynamic_update_slice_in_dim(carry, old + jnp.stack([key_part, value_part]), start, 1)
        return carry, query_part

    init = jnp.zeros((2, TOKENS + lead, KV, HD), jnp.float32)
    carry, query_parts = lax.scan(block_step, init, jnp.arange(N_SEQ, dtype=jnp.int32))
    query_grad = query_parts.reshape(TOKENS, HQ, HD).astype(jnp.bfloat16)
    key_grad = carry[0, lead:].astype(jnp.bfloat16)
    value_grad = carry[1, lead:].astype(jnp.bfloat16)
    return (gate_up_grad, route_grad, query_grad, key_grad, value_grad)
```

```python
import jax
import jax.numpy as jnp
from jax import lax
from jax.sharding import PartitionSpec as P

REACH = 7


masked_score = -1e30
highest = lax.Precision.HIGHEST


def passed_along(array, axis, by):
    count = lax.axis_size(axis)
    pairs = [(i, i + by) for i in range(count) if 0 <= i + by < count]
    return lax.ppermute(array, axis, pairs)


def attend(queries, upstream, keys_all, values_all, query_pos, key_pos, doc_begin, score_scale):
    scores = (
        jnp.einsum("tkgd,lkd->kgtl", queries, keys_all, preferred_element_type=jnp.float32)
        * score_scale
    )
    valid = (key_pos[None, :] <= query_pos[:, None]) & (key_pos[None, :] >= doc_begin[:, None])
    scores = jnp.where(valid[None, None], scores, masked_score)
    row_max = jnp.max(scores, axis=3, keepdims=True)
    exponent = jnp.exp(scores - row_max)
    probs = exponent / jnp.sum(exponent, axis=3, keepdims=True)
    dprob = jnp.einsum("tkgd,lkd->kgtl", upstream, values_all, preferred_element_type=jnp.float32)
    row_dot = jnp.sum(probs * dprob, axis=3, keepdims=True)
    probs_b = probs.astype(jnp.bfloat16)
    dscore = (probs * (dprob - row_dot)).astype(jnp.bfloat16)
    query_part = (
        jnp.einsum("kgtl,lkd->tkgd", dscore, keys_all, preferred_element_type=jnp.float32)
        * score_scale
    )
    key_part = (
        jnp.einsum("kgtl,tkgd->lkd", dscore, queries, preferred_element_type=jnp.float32)
        * score_scale
    )
    value_part = jnp.einsum("kgtl,tkgd->lkd", probs_b, upstream, preferred_element_type=jnp.float32)
    return (query_part, key_part, value_part)


def per_device(
    out_grad,
    expert_ids,
    top_logits,
    doc_start,
    router,
    w_down,
    saved_gu,
    out_weight,
    query,
    key,
    value,
):
    seq_count = lax.axis_size("seq")
    seq_index = lax.axis_index("seq")
    tokens_here = out_grad.shape[0]
    features = out_grad.shape[1]
    slots_all = saved_gu.shape[3]
    capacity = slots_all // seq_count
    experts = router.shape[0]
    top_count = expert_ids.shape[1]
    weights = jax.nn.softmax(top_logits, axis=1)
    hits = (expert_ids[:, :, None] == jnp.arange(experts, dtype=jnp.int32)[None, None, :]).astype(
        jnp.float32
    )
    per_token = jnp.sum(hits, axis=1)
    earlier = (jnp.arange(tokens_here)[:, None] > jnp.arange(tokens_here)[None, :]).astype(
        jnp.float32
    )
    before = jnp.dot(earlier, per_token, precision=highest)
    rank = jnp.sum(hits * before[:, None, :], axis=2).astype(jnp.int32)
    target = expert_ids * capacity + rank
    placed = (
        target[None, :, :] == jnp.arange(experts * capacity, dtype=jnp.int32)[:, None, None]
    ).astype(jnp.float32)
    pick = jnp.sum(placed, axis=2).astype(jnp.bfloat16)
    send_rows = jnp.dot(pick, out_grad, preferred_element_type=jnp.float32).astype(jnp.bfloat16)
    send_weight = jnp.sum(placed * weights[None, :, :], axis=(1, 2)).astype(jnp.bfloat16)
    weight_lanes = jnp.zeros((experts * capacity, 128), jnp.bfloat16).at[:, 0].set(send_weight)
    payload = jnp.concatenate([send_rows, weight_lanes], axis=1)
    weight_full = lax.all_gather(out_weight, "seq", axis=1, tiled=True)
    kv_heads = key.shape[1]
    head_dim = key.shape[2]
    group = query.shape[1] // kv_heads
    paired = jnp.stack([key, value])
    blocks = [paired]
    for distance in range(1, REACH + 1):
        blocks.append(passed_along(paired, "seq", distance))
    sent_payload = lax.all_to_all(
        payload.reshape(experts, capacity, features + 128),
        "seq",
        split_axis=0,
        concat_axis=0,
        tiled=True,
    ).reshape(slots_all, features + 128)
    sent_payload, weight_full, blocks = lax.optimization_barrier(
        (sent_payload, weight_full, tuple(blocks))
    )
    slot_rows = sent_payload[:, :features]
    sent_weight = sent_payload[:, features]
    weight_here = w_down[0]
    raw = lax.psum_scatter(
        lax.dot_general(
            weight_here, slot_rows, (((1,), (1,)), ((), ())), preferred_element_type=jnp.float32
        ).astype(jnp.bfloat16),
        "head",
        scatter_dimension=0,
        tiled=True,
    ).astype(jnp.float32)
    gate = saved_gu[0, 0].astype(jnp.float32)
    up = saved_gu[0, 1].astype(jnp.float32)
    sig = jax.nn.sigmoid(gate)
    act = gate * sig
    hidden = act * up
    slot_part = jnp.sum(hidden * raw, axis=0)
    scaled = raw * sent_weight.reshape(slots_all).astype(jnp.float32)[None, :]
    gate_up_grad = jnp.stack([scaled * up * sig * (1.0 + gate * (1.0 - sig)), scaled * act])[
        None
    ].astype(jnp.bfloat16)
    slot_grad = lax.psum(slot_part, "head")
    returned = lax.all_to_all(
        slot_grad.reshape(seq_count, capacity), "seq", split_axis=0, concat_axis=0, tiled=True
    )
    route_grad = jnp.take(returned.reshape(-1), target.reshape(-1)).reshape(tokens_here, top_count)
    logit_grad = weights * (route_grad - jnp.sum(weights * route_grad, axis=1, keepdims=True))
    dense = jnp.einsum("tk,tke->te", logit_grad, hits, precision=highest)
    router_term = jnp.dot(dense, router.astype(jnp.float32), precision=highest)
    input_slice = (out_grad.astype(jnp.float32) + router_term).astype(jnp.bfloat16)
    input_grad = lax.all_gather(input_slice, "head", axis=1, tiled=True)
    attn_grad = lax.dot_general(
        input_grad,
        weight_full,
        (((1,), (1,)), ((), ())),
        preferred_element_type=jnp.float32,
    ).astype(jnp.bfloat16)
    window = jnp.concatenate(blocks[::-1], axis=1)
    local_pos = jnp.arange(tokens_here, dtype=jnp.int32)
    key_pos = jnp.concatenate(
        [(seq_index - distance) * tokens_here + local_pos for distance in range(REACH, -1, -1)]
    )
    query_pos = seq_index * tokens_here + local_pos
    queries = query.reshape(tokens_here, kv_heads, group, head_dim)
    upstream = attn_grad.reshape(tokens_here, kv_heads, group, head_dim)
    query_part, key_part, value_part = attend(
        queries, upstream, window[0], window[1], query_pos, key_pos, doc_start, head_dim ** (-0.5)
    )
    query_grad = query_part.reshape(query.shape).astype(jnp.bfloat16)
    pieces = jnp.stack([key_part, value_part]).reshape(
        2, REACH + 1, tokens_here, kv_heads, head_dim
    )
    totals = pieces[:, REACH]
    for distance in range(1, REACH + 1):
        totals = totals + passed_along(
            pieces[:, REACH - distance].astype(jnp.bfloat16), "seq", -distance
        ).astype(jnp.float32)
    return (
        gate_up_grad,
        route_grad,
        query_grad,
        totals[0].astype(jnp.bfloat16),
        totals[1].astype(jnp.bfloat16),
    )


def solution(mesh):
    in_specs = (
        P("seq", "head"),
        P("seq", None),
        P("seq", None),
        P("seq"),
        P(None, "head"),
        P("seq", None, "head"),
        P("seq", None, "head", None),
        P("head", "seq"),
        P("seq", "head", None),
        P("seq", "head", None),
        P("seq", "head", None),
    )
    out_specs = (
        P("seq", None, "head", None),
        P("seq", None),
        P("seq", "head", None),
        P("seq", "head", None),
        P("seq", "head", None),
    )
    return jax.shard_map(
        per_device, mesh=mesh, in_specs=in_specs, out_specs=out_specs, check_vma=False
    )
```

```python
import jax
import jax.numpy as jnp
from jax import lax
from jax.sharding import PartitionSpec as P

REACH = 7


masked_score = -1e30
highest = lax.Precision.HIGHEST


def passed_along(array, axis, by):
    count = lax.axis_size(axis)
    pairs = [(i, i + by) for i in range(count) if 0 <= i + by < count]
    return lax.ppermute(array, axis, pairs)


def attend(queries, upstream, keys_all, values_all, query_pos, key_pos, doc_begin, score_scale):
    scores = (
        jnp.einsum("tkgd,lkd->kgtl", queries, keys_all, preferred_element_type=jnp.float32)
        * score_scale
    )
    valid = (key_pos[None, :] <= query_pos[:, None]) & (key_pos[None, :] >= doc_begin[:, None])
    scores = jnp.where(valid[None, None], scores, masked_score)
    row_max = jnp.max(scores, axis=3, keepdims=True)
    exponent = jnp.exp(scores - row_max)
    probs = exponent / jnp.sum(exponent, axis=3, keepdims=True)
    dprob = jnp.einsum("tkgd,lkd->kgtl", upstream, values_all, preferred_element_type=jnp.float32)
    row_dot = jnp.sum(probs * dprob, axis=3, keepdims=True)
    probs_b = probs.astype(jnp.bfloat16)
    dscore = (probs * (dprob - row_dot)).astype(jnp.bfloat16)
    query_part = (
        jnp.einsum("kgtl,lkd->tkgd", dscore, keys_all, preferred_element_type=jnp.float32)
        * score_scale
    )
    key_part = (
        jnp.einsum("kgtl,tkgd->lkd", dscore, queries, preferred_element_type=jnp.float32)
        * score_scale
    )
    value_part = jnp.einsum("kgtl,tkgd->lkd", probs_b, upstream, preferred_element_type=jnp.float32)
    return (query_part, key_part, value_part)


def per_device(
    out_grad,
    expert_ids,
    top_logits,
    doc_start,
    router,
    w_down,
    saved_gu,
    out_weight,
    query,
    key,
    value,
):
    seq_count = lax.axis_size("seq")
    seq_index = lax.axis_index("seq")
    tokens_here = out_grad.shape[0]
    features = out_grad.shape[1]
    slots_all = saved_gu.shape[3]
    capacity = slots_all // seq_count
    experts = router.shape[0]
    top_count = expert_ids.shape[1]
    weights = jax.nn.softmax(top_logits, axis=1)
    hits = (expert_ids[:, :, None] == jnp.arange(experts, dtype=jnp.int32)[None, None, :]).astype(
        jnp.float32
    )
    per_token = jnp.sum(hits, axis=1)
    earlier = (jnp.arange(tokens_here)[:, None] > jnp.arange(tokens_here)[None, :]).astype(
        jnp.float32
    )
    before = jnp.dot(earlier, per_token, precision=highest)
    rank = jnp.sum(hits * before[:, None, :], axis=2).astype(jnp.int32)
    target = expert_ids * capacity + rank
    placed = (
        target[None, :, :] == jnp.arange(experts * capacity, dtype=jnp.int32)[:, None, None]
    ).astype(jnp.float32)
    pick = jnp.sum(placed, axis=2).astype(jnp.bfloat16)
    send_rows = jnp.dot(pick, out_grad, preferred_element_type=jnp.float32).astype(jnp.bfloat16)
    send_weight = jnp.sum(placed * weights[None, :, :], axis=(1, 2)).astype(jnp.bfloat16)
    weight_lanes = jnp.zeros((experts * capacity, 128), jnp.bfloat16).at[:, 0].set(send_weight)
    payload = jnp.concatenate([send_rows, weight_lanes], axis=1)
    weight_full = out_weight
    kv_heads = key.shape[1]
    head_dim = key.shape[2]
    group = query.shape[1] // kv_heads
    paired = jnp.stack([key, value])
    blocks = [paired]
    for distance in range(1, REACH + 1):
        blocks.append(passed_along(paired, "seq", distance))
    sent_payload = lax.all_to_all(
        payload.reshape(experts, capacity, features + 128),
        "seq",
        split_axis=0,
        concat_axis=0,
        tiled=True,
    ).reshape(slots_all, features + 128)
    sent_payload, weight_full, blocks = lax.optimization_barrier(
        (sent_payload, weight_full, tuple(blocks))
    )
    slot_rows = sent_payload[:, :features]
    sent_weight = sent_payload[:, features]
    weight_here = w_down[0]
    raw = lax.psum_scatter(
        lax.dot_general(
            weight_here, slot_rows, (((1,), (1,)), ((), ())), preferred_element_type=jnp.float32
        ).astype(jnp.bfloat16),
        "head",
        scatter_dimension=0,
        tiled=True,
    ).astype(jnp.float32)
    gate = saved_gu[0, 0].astype(jnp.float32)
    up = saved_gu[0, 1].astype(jnp.float32)
    sig = jax.nn.sigmoid(gate)
    act = gate * sig
    hidden = act * up
    slot_part = jnp.sum(hidden * raw, axis=0)
    scaled = raw * sent_weight.reshape(slots_all).astype(jnp.float32)[None, :]
    gate_up_grad = jnp.stack([scaled * up * sig * (1.0 + gate * (1.0 - sig)), scaled * act])[
        None
    ].astype(jnp.bfloat16)
    slot_grad = lax.psum(slot_part, "head")
    returned = lax.all_to_all(
        slot_grad.reshape(seq_count, capacity), "seq", split_axis=0, concat_axis=0, tiled=True
    )
    route_grad = jnp.take(returned.reshape(-1), target.reshape(-1)).reshape(tokens_here, top_count)
    logit_grad = weights * (route_grad - jnp.sum(weights * route_grad, axis=1, keepdims=True))
    dense = jnp.einsum("tk,tke->te", logit_grad, hits, precision=highest)
    router_term = jnp.dot(dense, router.astype(jnp.float32), precision=highest)
    input_slice = (out_grad.astype(jnp.float32) + router_term).astype(jnp.bfloat16)
    input_grad = lax.all_gather(input_slice, "head", axis=1, tiled=True)
    core = seq_index % 2
    by_parity = input_grad.reshape(tokens_here, seq_count // 2, 2, -1)
    mine = lax.dynamic_index_in_dim(by_parity, core, axis=2, keepdims=False)
    theirs = lax.dynamic_index_in_dim(by_parity, 1 - core, axis=2, keepdims=False)
    ordered = jnp.concatenate(
        [mine.reshape(tokens_here, -1), theirs.reshape(tokens_here, -1)], axis=1
    )
    attn_grad = lax.dot_general(
        ordered,
        weight_full,
        (((1,), (1,)), ((), ())),
        preferred_element_type=jnp.float32,
    ).astype(jnp.bfloat16)
    window = jnp.concatenate(blocks[::-1], axis=1)
    local_pos = jnp.arange(tokens_here, dtype=jnp.int32)
    key_pos = jnp.concatenate(
        [(seq_index - distance) * tokens_here + local_pos for distance in range(REACH, -1, -1)]
    )
    query_pos = seq_index * tokens_here + local_pos
    queries = query.reshape(tokens_here, kv_heads, group, head_dim)
    upstream = attn_grad.reshape(tokens_here, kv_heads, group, head_dim)
    query_part, key_part, value_part = attend(
        queries, upstream, window[0], window[1], query_pos, key_pos, doc_start, head_dim ** (-0.5)
    )
    query_grad = query_part.reshape(query.shape).astype(jnp.bfloat16)
    pieces = jnp.stack([key_part, value_part]).reshape(
        2, REACH + 1, tokens_here, kv_heads, head_dim
    )
    totals = pieces[:, REACH]
    for distance in range(1, REACH + 1):
        totals = totals + passed_along(
            pieces[:, REACH - distance].astype(jnp.bfloat16), "seq", -distance
        ).astype(jnp.float32)
    return (
        gate_up_grad,
        route_grad,
        query_grad,
        totals[0].astype(jnp.bfloat16),
        totals[1].astype(jnp.bfloat16),
    )


def gather_columns(out_weight):
    half = lax.all_gather(out_weight, "chip", axis=1, tiled=True)
    other = lax.ppermute(half, "core", [(0, 1), (1, 0)])
    return jnp.concatenate([half, other], axis=1)


def solution(mesh):
    chips = mesh.devices.shape[0] // 2
    split_mesh = jax.sharding.Mesh(
        mesh.devices.reshape(chips, 2, mesh.devices.shape[1]), ("chip", "core", "head")
    )
    gather = jax.shard_map(
        gather_columns,
        mesh=split_mesh,
        in_specs=P("head", ("chip", "core")),
        out_specs=P("head", ("chip", "core")),
        check_vma=False,
    )
    in_specs = (
        P("seq", "head"),
        P("seq", None),
        P("seq", None),
        P("seq"),
        P(None, "head"),
        P("seq", None, "head"),
        P("seq", None, "head", None),
        P("head", "seq"),
        P("seq", "head", None),
        P("seq", "head", None),
        P("seq", "head", None),
    )
    out_specs = (
        P("seq", None, "head", None),
        P("seq", None),
        P("seq", "head", None),
        P("seq", "head", None),
        P("seq", "head", None),
    )
    body = jax.shard_map(
        per_device, mesh=mesh, in_specs=in_specs, out_specs=out_specs, check_vma=False
    )

    def run(*args):
        args = list(args)
        args[7] = gather(args[7])
        return body(*args)

    return run
```

```python
import jax
import jax.numpy as jnp
from jax import lax
from jax.sharding import PartitionSpec as P

REACH = 7


masked_score = -1e30
highest = lax.Precision.HIGHEST


def passed_along(array, axis, by):
    count = lax.axis_size(axis)
    pairs = [(i, i + by) for i in range(count) if 0 <= i + by < count]
    return lax.ppermute(array, axis, pairs)


def attend(queries, upstream, keys_all, values_all, query_pos, key_pos, doc_begin, score_scale):
    scores = (
        jnp.einsum("tkgd,lkd->kgtl", queries, keys_all, preferred_element_type=jnp.float32)
        * score_scale
    )
    valid = (key_pos[None, :] <= query_pos[:, None]) & (key_pos[None, :] >= doc_begin[:, None])
    scores = jnp.where(valid[None, None], scores, masked_score)
    row_max = jnp.max(scores, axis=3, keepdims=True)
    exponent = jnp.exp(scores - row_max)
    probs = exponent / jnp.sum(exponent, axis=3, keepdims=True)
    dprob = jnp.einsum("tkgd,lkd->kgtl", upstream, values_all, preferred_element_type=jnp.float32)
    row_dot = jnp.sum(probs * dprob, axis=3, keepdims=True)
    probs_b = probs.astype(jnp.bfloat16)
    dscore = (probs * (dprob - row_dot)).astype(jnp.bfloat16)
    query_part = (
        jnp.einsum("kgtl,lkd->tkgd", dscore, keys_all, preferred_element_type=jnp.float32)
        * score_scale
    )
    key_part = (
        jnp.einsum("kgtl,tkgd->lkd", dscore, queries, preferred_element_type=jnp.float32)
        * score_scale
    )
    value_part = jnp.einsum("kgtl,tkgd->lkd", probs_b, upstream, preferred_element_type=jnp.float32)
    return (query_part, key_part, value_part)


def per_device(
    out_grad,
    expert_ids,
    top_logits,
    doc_start,
    router,
    w_down,
    saved_gu,
    out_weight,
    query,
    key,
    value,
):
    seq_count = lax.axis_size("seq")
    seq_index = lax.axis_index("seq")
    tokens_here = out_grad.shape[0]
    features = out_grad.shape[1]
    slots_all = saved_gu.shape[3]
    capacity = slots_all // seq_count
    experts = router.shape[0]
    top_count = expert_ids.shape[1]
    weights = jax.nn.softmax(top_logits, axis=1)
    hits = (expert_ids[:, :, None] == jnp.arange(experts, dtype=jnp.int32)[None, None, :]).astype(
        jnp.float32
    )
    per_token = jnp.sum(hits, axis=1)
    earlier = (jnp.arange(tokens_here)[:, None] > jnp.arange(tokens_here)[None, :]).astype(
        jnp.float32
    )
    before = jnp.dot(earlier, per_token, precision=highest)
    rank = jnp.sum(hits * before[:, None, :], axis=2).astype(jnp.int32)
    target = expert_ids * capacity + rank
    pad = -(-(capacity + 1) // 16) * 16
    padded_target = (expert_ids * pad + rank).reshape(-1)
    onehot = padded_target[None, :] == jnp.arange(experts * pad, dtype=jnp.int32)[:, None]
    token_of = (
        jnp.arange(tokens_here * top_count, dtype=jnp.int32)[:, None] // top_count
        == jnp.arange(tokens_here, dtype=jnp.int32)[None, :]
    ).astype(jnp.bfloat16)
    pick = jnp.dot(
        onehot.astype(jnp.bfloat16), token_of, preferred_element_type=jnp.float32
    ).astype(jnp.bfloat16)
    send_rows = jnp.dot(pick, out_grad, preferred_element_type=jnp.float32)
    send_weight = jnp.sum(jnp.where(onehot, weights.reshape(-1)[None, :], 0.0), axis=1)
    weight_plane = (
        jnp.zeros((experts, pad, features), jnp.float32)
        .at[:, capacity, :pad]
        .set(send_weight.reshape(experts, pad))
    )
    payload = (send_rows.reshape(experts, pad, features) + weight_plane).astype(jnp.bfloat16)
    weight_full = lax.all_gather(out_weight, "seq", axis=1, tiled=True)
    kv_heads = key.shape[1]
    head_dim = key.shape[2]
    group = query.shape[1] // kv_heads
    paired = jnp.stack([key, value])
    blocks = [paired]
    for distance in range(1, REACH + 1):
        blocks.append(passed_along(paired, "seq", distance))
    sent_payload = lax.all_to_all(payload, "seq", split_axis=0, concat_axis=0, tiled=True)
    sent_payload, weight_full, blocks = lax.optimization_barrier(
        (sent_payload, weight_full, tuple(blocks))
    )
    slot_rows = sent_payload[:, :capacity, :].reshape(slots_all, features)
    sent_weight = sent_payload[:, capacity, :capacity].reshape(slots_all)
    weight_here = w_down[0]
    raw = lax.psum_scatter(
        lax.dot_general(
            weight_here, slot_rows, (((1,), (1,)), ((), ())), preferred_element_type=jnp.float32
        ).astype(jnp.bfloat16),
        "head",
        scatter_dimension=0,
        tiled=True,
    ).astype(jnp.float32)
    gate = saved_gu[0, 0].astype(jnp.float32)
    up = saved_gu[0, 1].astype(jnp.float32)
    sig = jax.nn.sigmoid(gate)
    act = gate * sig
    hidden = act * up
    slot_part = jnp.sum(hidden * raw, axis=0)
    scaled = raw * sent_weight.reshape(slots_all).astype(jnp.float32)[None, :]
    gate_up_grad = jnp.stack([scaled * up * sig * (1.0 + gate * (1.0 - sig)), scaled * act])[
        None
    ].astype(jnp.bfloat16)
    slot_grad = lax.psum(slot_part, "head")
    returned = lax.all_to_all(
        slot_grad.reshape(seq_count, capacity), "seq", split_axis=0, concat_axis=0, tiled=True
    )
    route_grad = jnp.take(returned.reshape(-1), target.reshape(-1)).reshape(tokens_here, top_count)
    logit_grad = weights * (route_grad - jnp.sum(weights * route_grad, axis=1, keepdims=True))
    dense = jnp.einsum("tk,tke->te", logit_grad, hits, precision=highest)
    router_term = jnp.dot(dense, router.astype(jnp.float32), precision=highest)
    input_slice = (out_grad.astype(jnp.float32) + router_term).astype(jnp.bfloat16)
    input_grad = lax.all_gather(input_slice, "head", axis=1, tiled=True)
    attn_grad = lax.dot_general(
        input_grad,
        weight_full,
        (((1,), (1,)), ((), ())),
        preferred_element_type=jnp.float32,
    ).astype(jnp.bfloat16)
    window = jnp.concatenate(blocks[::-1], axis=1)
    local_pos = jnp.arange(tokens_here, dtype=jnp.int32)
    key_pos = jnp.concatenate(
        [(seq_index - distance) * tokens_here + local_pos for distance in range(REACH, -1, -1)]
    )
    query_pos = seq_index * tokens_here + local_pos
    queries = query.reshape(tokens_here, kv_heads, group, head_dim)
    upstream = attn_grad.reshape(tokens_here, kv_heads, group, head_dim)
    query_part, key_part, value_part = attend(
        queries, upstream, window[0], window[1], query_pos, key_pos, doc_start, head_dim ** (-0.5)
    )
    query_grad = query_part.reshape(query.shape).astype(jnp.bfloat16)
    pieces = jnp.stack([key_part, value_part]).reshape(
        2, REACH + 1, tokens_here, kv_heads, head_dim
    )
    totals = pieces[:, REACH]
    for distance in range(1, REACH + 1):
        totals = totals + passed_along(
            pieces[:, REACH - distance].astype(jnp.bfloat16), "seq", -distance
        ).astype(jnp.float32)
    return (
        gate_up_grad,
        route_grad,
        query_grad,
        totals[0].astype(jnp.bfloat16),
        totals[1].astype(jnp.bfloat16),
    )


def solution(mesh):
    in_specs = (
        P("seq", "head"),
        P("seq", None),
        P("seq", None),
        P("seq"),
        P(None, "head"),
        P("seq", None, "head"),
        P("seq", None, "head", None),
        P("head", "seq"),
        P("seq", "head", None),
        P("seq", "head", None),
        P("seq", "head", None),
    )
    out_specs = (
        P("seq", None, "head", None),
        P("seq", None),
        P("seq", "head", None),
        P("seq", "head", None),
        P("seq", "head", None),
    )
    return jax.shard_map(
        per_device, mesh=mesh, in_specs=in_specs, out_specs=out_specs, check_vma=False
    )
```

```python
import jax
import jax.numpy as jnp
from jax import lax
from jax.sharding import PartitionSpec as P

REACH = 7


masked_score = -1e30
highest = lax.Precision.HIGHEST


def passed_along(array, axis, by):
    count = lax.axis_size(axis)
    pairs = [(i, i + by) for i in range(count) if 0 <= i + by < count]
    return lax.ppermute(array, axis, pairs)


def head_sum(part):
    count = lax.axis_size("head")
    step = 1
    while step < count:
        pairs = [(i, i ^ step) for i in range(count)]
        part = part + lax.ppermute(part, "head", pairs)
        step *= 2
    return part


def attend(queries, upstream, keys_all, values_all, query_pos, key_pos, doc_begin, score_scale):
    scores = (
        jnp.einsum("tkgd,lkd->kgtl", queries, keys_all, preferred_element_type=jnp.float32)
        * score_scale
    )
    valid = (key_pos[None, :] <= query_pos[:, None]) & (key_pos[None, :] >= doc_begin[:, None])
    scores = jnp.where(valid[None, None], scores, masked_score)
    row_max = jnp.max(scores, axis=3, keepdims=True)
    exponent = jnp.exp(scores - row_max)
    probs = exponent / jnp.sum(exponent, axis=3, keepdims=True)
    dprob = jnp.einsum("tkgd,lkd->kgtl", upstream, values_all, preferred_element_type=jnp.float32)
    row_dot = jnp.sum(probs * dprob, axis=3, keepdims=True)
    probs_b = probs.astype(jnp.bfloat16)
    dscore = (probs * (dprob - row_dot)).astype(jnp.bfloat16)
    query_part = (
        jnp.einsum("kgtl,lkd->tkgd", dscore, keys_all, preferred_element_type=jnp.float32)
        * score_scale
    )
    key_part = (
        jnp.einsum("kgtl,tkgd->lkd", dscore, queries, preferred_element_type=jnp.float32)
        * score_scale
    )
    value_part = jnp.einsum("kgtl,tkgd->lkd", probs_b, upstream, preferred_element_type=jnp.float32)
    return (query_part, key_part, value_part)


def per_device(
    out_grad,
    expert_ids,
    top_logits,
    doc_start,
    router,
    w_down,
    saved_gu,
    out_weight,
    query,
    key,
    value,
):
    seq_count = lax.axis_size("seq")
    seq_index = lax.axis_index("seq")
    tokens_here = out_grad.shape[0]
    features = out_grad.shape[1]
    slots_all = saved_gu.shape[3]
    capacity = slots_all // seq_count
    experts = router.shape[0]
    top_count = expert_ids.shape[1]
    weights = jax.nn.softmax(top_logits, axis=1)
    hits = (expert_ids[:, :, None] == jnp.arange(experts, dtype=jnp.int32)[None, None, :]).astype(
        jnp.float32
    )
    per_token = jnp.sum(hits, axis=1)
    earlier = (jnp.arange(tokens_here)[:, None] > jnp.arange(tokens_here)[None, :]).astype(
        jnp.float32
    )
    before = jnp.dot(earlier, per_token, precision=highest)
    rank = jnp.sum(hits * before[:, None, :], axis=2).astype(jnp.int32)
    target = expert_ids * capacity + rank
    pad = -(-(capacity + 1) // 16) * 16
    padded_target = (expert_ids * pad + rank).reshape(-1)
    onehot = padded_target[None, :] == jnp.arange(experts * pad, dtype=jnp.int32)[:, None]
    token_of = (
        jnp.arange(tokens_here * top_count, dtype=jnp.int32)[:, None] // top_count
        == jnp.arange(tokens_here, dtype=jnp.int32)[None, :]
    ).astype(jnp.bfloat16)
    pick = jnp.dot(
        onehot.astype(jnp.bfloat16), token_of, preferred_element_type=jnp.float32
    ).astype(jnp.bfloat16)
    send_rows = jnp.dot(pick, out_grad, preferred_element_type=jnp.float32)
    send_weight = jnp.sum(jnp.where(onehot, weights.reshape(-1)[None, :], 0.0), axis=1)
    weight_row = jnp.pad(send_weight.reshape(experts, pad), ((0, 0), (0, features - pad)))
    is_weight = (jnp.arange(pad) == capacity)[None, :, None]
    payload = jnp.where(
        is_weight, weight_row[:, None, :], send_rows.reshape(experts, pad, features)
    ).astype(jnp.bfloat16)
    weight_full = lax.all_gather(out_weight, "seq", axis=1, tiled=True)
    kv_heads = key.shape[1]
    head_dim = key.shape[2]
    group = query.shape[1] // kv_heads
    paired = jnp.stack([key, value])
    blocks = [paired]
    for distance in range(1, REACH + 1):
        blocks.append(passed_along(paired, "seq", distance))
    sent_payload = lax.all_to_all(payload, "seq", split_axis=0, concat_axis=0, tiled=True)
    sent_payload, weight_full, blocks = lax.optimization_barrier(
        (sent_payload, weight_full, tuple(blocks))
    )
    slot_rows = sent_payload[:, :capacity, :].reshape(slots_all, features)
    sent_weight = sent_payload[:, capacity, :capacity].reshape(slots_all)
    weight_here = w_down[0]
    raw = lax.psum_scatter(
        lax.dot_general(
            weight_here, slot_rows, (((1,), (1,)), ((), ())), preferred_element_type=jnp.float32
        ).astype(jnp.bfloat16),
        "head",
        scatter_dimension=0,
        tiled=True,
    ).astype(jnp.float32)
    gate = saved_gu[0, 0].astype(jnp.float32)
    up = saved_gu[0, 1].astype(jnp.float32)
    sig = jax.nn.sigmoid(gate)
    act = gate * sig
    hidden = act * up
    slot_part = jnp.sum(hidden * raw, axis=0)
    scaled = raw * sent_weight.reshape(slots_all).astype(jnp.float32)[None, :]
    gate_up_grad = jnp.stack([scaled * up * sig * (1.0 + gate * (1.0 - sig)), scaled * act])[
        None
    ].astype(jnp.bfloat16)
    slot_grad = head_sum(slot_part)
    returned = lax.all_to_all(
        slot_grad.reshape(seq_count, capacity), "seq", split_axis=0, concat_axis=0, tiled=True
    )
    route_grad = jnp.take(returned.reshape(-1), target.reshape(-1)).reshape(tokens_here, top_count)
    logit_grad = weights * (route_grad - jnp.sum(weights * route_grad, axis=1, keepdims=True))
    dense = jnp.einsum("tk,tke->te", logit_grad, hits, precision=highest)
    router_term = jnp.dot(dense, router.astype(jnp.float32), precision=highest)
    input_slice = (out_grad.astype(jnp.float32) + router_term).astype(jnp.bfloat16)
    input_grad = lax.all_gather(input_slice, "head", axis=1, tiled=True)
    attn_grad = lax.dot_general(
        input_grad,
        weight_full,
        (((1,), (1,)), ((), ())),
        preferred_element_type=jnp.float32,
    ).astype(jnp.bfloat16)
    window = jnp.concatenate(blocks[::-1], axis=1)
    local_pos = jnp.arange(tokens_here, dtype=jnp.int32)
    key_pos = jnp.concatenate(
        [(seq_index - distance) * tokens_here + local_pos for distance in range(REACH, -1, -1)]
    )
    query_pos = seq_index * tokens_here + local_pos
    queries = query.reshape(tokens_here, kv_heads, group, head_dim)
    upstream = attn_grad.reshape(tokens_here, kv_heads, group, head_dim)
    query_part, key_part, value_part = attend(
        queries, upstream, window[0], window[1], query_pos, key_pos, doc_start, head_dim ** (-0.5)
    )
    query_grad = query_part.reshape(query.shape).astype(jnp.bfloat16)
    pieces = jnp.stack([key_part, value_part]).reshape(
        2, REACH + 1, tokens_here, kv_heads, head_dim
    )
    totals = pieces[:, REACH]
    for distance in range(1, REACH + 1):
        totals = totals + passed_along(
            pieces[:, REACH - distance].astype(jnp.bfloat16), "seq", -distance
        ).astype(jnp.float32)
    return (
        gate_up_grad,
        route_grad,
        query_grad,
        totals[0].astype(jnp.bfloat16),
        totals[1].astype(jnp.bfloat16),
    )


def solution(mesh):
    in_specs = (
        P("seq", "head"),
        P("seq", None),
        P("seq", None),
        P("seq"),
        P(None, "head"),
        P("seq", None, "head"),
        P("seq", None, "head", None),
        P("head", "seq"),
        P("seq", "head", None),
        P("seq", "head", None),
        P("seq", "head", None),
    )
    out_specs = (
        P("seq", None, "head", None),
        P("seq", None),
        P("seq", "head", None),
        P("seq", "head", None),
        P("seq", "head", None),
    )
    return jax.shard_map(
        per_device, mesh=mesh, in_specs=in_specs, out_specs=out_specs, check_vma=False
    )
```

```python
import jax
import jax.numpy as jnp
from jax import lax
from jax.sharding import PartitionSpec as P

REACH = 7


masked_score = -1e30
highest = lax.Precision.HIGHEST


def passed_along(array, axis, by):
    count = lax.axis_size(axis)
    pairs = [(i, i + by) for i in range(count) if 0 <= i + by < count]
    return lax.ppermute(array, axis, pairs)


def head_sum(part):
    count = lax.axis_size("head")
    step = 1
    while step < count:
        pairs = [(i, i ^ step) for i in range(count)]
        part = part + lax.ppermute(part, "head", pairs)
        step *= 2
    return part


def attend(queries, upstream, keys_all, values_all, query_pos, key_pos, doc_begin, score_scale):
    scores = (
        jnp.einsum("tkgd,lkd->kgtl", queries, keys_all, preferred_element_type=jnp.float32)
        * score_scale
    )
    valid = (key_pos[None, :] <= query_pos[:, None]) & (key_pos[None, :] >= doc_begin[:, None])
    scores = jnp.where(valid[None, None], scores, masked_score)
    row_max = jnp.max(scores, axis=3, keepdims=True)
    exponent = jnp.exp(scores - row_max)
    probs = exponent / jnp.sum(exponent, axis=3, keepdims=True)
    dprob = jnp.einsum("tkgd,lkd->kgtl", upstream, values_all, preferred_element_type=jnp.float32)
    row_dot = jnp.sum(probs * dprob, axis=3, keepdims=True)
    probs_b = probs.astype(jnp.bfloat16)
    dscore = (probs * (dprob - row_dot)).astype(jnp.bfloat16)
    query_part = (
        jnp.einsum("kgtl,lkd->tkgd", dscore, keys_all, preferred_element_type=jnp.float32)
        * score_scale
    )
    key_part = (
        jnp.einsum("kgtl,tkgd->lkd", dscore, queries, preferred_element_type=jnp.float32)
        * score_scale
    )
    value_part = jnp.einsum("kgtl,tkgd->lkd", probs_b, upstream, preferred_element_type=jnp.float32)
    return (query_part, key_part, value_part)


def per_device(
    out_grad,
    expert_ids,
    top_logits,
    doc_start,
    router,
    w_down,
    saved_gu,
    out_weight,
    query,
    key,
    value,
):
    seq_count = lax.axis_size("seq")
    seq_index = lax.axis_index("seq")
    tokens_here = out_grad.shape[0]
    features = out_grad.shape[1]
    slots_all = saved_gu.shape[3]
    capacity = slots_all // seq_count
    experts = router.shape[0]
    top_count = expert_ids.shape[1]
    weights = jax.nn.softmax(top_logits, axis=1)
    hits = (expert_ids[:, :, None] == jnp.arange(experts, dtype=jnp.int32)[None, None, :]).astype(
        jnp.float32
    )
    per_token = jnp.sum(hits, axis=1)
    earlier = (jnp.arange(tokens_here)[:, None] > jnp.arange(tokens_here)[None, :]).astype(
        jnp.float32
    )
    before = jnp.dot(earlier, per_token, precision=highest)
    rank = jnp.sum(hits * before[:, None, :], axis=2).astype(jnp.int32)
    target = expert_ids * capacity + rank
    pad = -(-(capacity + 1) // 16) * 16
    padded_target = (expert_ids * pad + rank).reshape(-1)
    onehot = padded_target[None, :] == jnp.arange(experts * pad, dtype=jnp.int32)[:, None]
    token_of = (
        jnp.arange(tokens_here * top_count, dtype=jnp.int32)[:, None] // top_count
        == jnp.arange(tokens_here, dtype=jnp.int32)[None, :]
    ).astype(jnp.bfloat16)
    pick = jnp.dot(
        onehot.astype(jnp.bfloat16), token_of, preferred_element_type=jnp.float32
    ).astype(jnp.bfloat16)
    send_rows = jnp.dot(pick, out_grad, preferred_element_type=jnp.float32)
    send_weight = jnp.sum(jnp.where(onehot, weights.reshape(-1)[None, :], 0.0), axis=1)
    weight_row = jnp.pad(send_weight.reshape(experts, pad), ((0, 0), (0, features - pad)))
    is_weight = (jnp.arange(pad) == capacity)[None, :, None]
    payload = jnp.where(
        is_weight, weight_row[:, None, :], send_rows.reshape(experts, pad, features)
    ).astype(jnp.bfloat16)
    weight_full = lax.all_gather(out_weight, "seq", axis=1, tiled=True)
    kv_heads = key.shape[1]
    head_dim = key.shape[2]
    group = query.shape[1] // kv_heads
    paired = jnp.stack([key, value])
    blocks = [paired]
    for distance in range(1, REACH + 1):
        blocks.append(passed_along(paired, "seq", distance))
    sent_payload = lax.all_to_all(payload, "seq", split_axis=0, concat_axis=0, tiled=True)
    sent_payload, blocks = lax.optimization_barrier((sent_payload, tuple(blocks)))
    slot_rows = sent_payload[:, :capacity, :].reshape(slots_all, features)
    sent_weight = sent_payload[:, capacity, :capacity].reshape(slots_all)
    weight_here = w_down[0]
    head_count = lax.axis_size("head")
    partial = lax.dot_general(
        weight_here, slot_rows, (((1,), (1,)), ((), ())), preferred_element_type=jnp.float32
    ).astype(jnp.bfloat16)
    received = lax.all_to_all(
        partial.reshape(head_count, -1, slots_all), "head", split_axis=0, concat_axis=0, tiled=True
    )
    raw = jnp.sum(received.astype(jnp.float32), axis=0)
    gate = saved_gu[0, 0].astype(jnp.float32)
    up = saved_gu[0, 1].astype(jnp.float32)
    sig = jax.nn.sigmoid(gate)
    act = gate * sig
    hidden = act * up
    slot_part = jnp.sum(hidden * raw, axis=0)
    scaled = raw * sent_weight.reshape(slots_all).astype(jnp.float32)[None, :]
    gate_up_grad = jnp.stack([scaled * up * sig * (1.0 + gate * (1.0 - sig)), scaled * act])[
        None
    ].astype(jnp.bfloat16)
    slot_part, weight_full = lax.optimization_barrier((slot_part, weight_full))
    slot_grad = head_sum(slot_part)
    returned = lax.all_to_all(
        slot_grad.reshape(seq_count, capacity), "seq", split_axis=0, concat_axis=0, tiled=True
    )
    route_grad = jnp.take(returned.reshape(-1), target.reshape(-1)).reshape(tokens_here, top_count)
    logit_grad = weights * (route_grad - jnp.sum(weights * route_grad, axis=1, keepdims=True))
    dense = jnp.einsum("tk,tke->te", logit_grad, hits, precision=highest)
    router_term = jnp.dot(dense, router.astype(jnp.float32), precision=highest)
    input_slice = (out_grad.astype(jnp.float32) + router_term).astype(jnp.bfloat16)
    input_grad = lax.all_gather(input_slice, "head", axis=1, tiled=True)
    attn_grad = lax.dot_general(
        input_grad,
        weight_full,
        (((1,), (1,)), ((), ())),
        preferred_element_type=jnp.float32,
    ).astype(jnp.bfloat16)
    window = jnp.concatenate(blocks[::-1], axis=1)
    local_pos = jnp.arange(tokens_here, dtype=jnp.int32)
    key_pos = jnp.concatenate(
        [(seq_index - distance) * tokens_here + local_pos for distance in range(REACH, -1, -1)]
    )
    query_pos = seq_index * tokens_here + local_pos
    queries = query.reshape(tokens_here, kv_heads, group, head_dim)
    upstream = attn_grad.reshape(tokens_here, kv_heads, group, head_dim)
    query_part, key_part, value_part = attend(
        queries, upstream, window[0], window[1], query_pos, key_pos, doc_start, head_dim ** (-0.5)
    )
    query_grad = query_part.reshape(query.shape).astype(jnp.bfloat16)
    pieces = jnp.stack([key_part, value_part]).reshape(
        2, REACH + 1, tokens_here, kv_heads, head_dim
    )
    totals = pieces[:, REACH]
    for distance in range(1, REACH + 1):
        totals = totals + passed_along(
            pieces[:, REACH - distance].astype(jnp.bfloat16), "seq", -distance
        ).astype(jnp.float32)
    return (
        gate_up_grad,
        route_grad,
        query_grad,
        totals[0].astype(jnp.bfloat16),
        totals[1].astype(jnp.bfloat16),
    )


def solution(mesh):
    in_specs = (
        P("seq", "head"),
        P("seq", None),
        P("seq", None),
        P("seq"),
        P(None, "head"),
        P("seq", None, "head"),
        P("seq", None, "head", None),
        P("head", "seq"),
        P("seq", "head", None),
        P("seq", "head", None),
        P("seq", "head", None),
    )
    out_specs = (
        P("seq", None, "head", None),
        P("seq", None),
        P("seq", "head", None),
        P("seq", "head", None),
        P("seq", "head", None),
    )
    return jax.shard_map(
        per_device, mesh=mesh, in_specs=in_specs, out_specs=out_specs, check_vma=False
    )
```

```python
import jax
import jax.numpy as jnp
from jax import lax
from jax.sharding import PartitionSpec as P

REACH = 7


masked_score = -1e30
highest = lax.Precision.HIGHEST


def passed_along(array, axis, by):
    count = lax.axis_size(axis)
    pairs = [(i, i + by) for i in range(count) if 0 <= i + by < count]
    return lax.ppermute(array, axis, pairs)


def head_sum(part):
    count = lax.axis_size("head")
    step = 1
    while step < count:
        pairs = [(i, i ^ step) for i in range(count)]
        part = part + lax.ppermute(part, "head", pairs)
        step *= 2
    return part


def attend(queries, upstream, keys_all, values_all, query_pos, key_pos, doc_begin, score_scale):
    scores = (
        jnp.einsum("tkgd,lkd->kgtl", queries, keys_all, preferred_element_type=jnp.float32)
        * score_scale
    )
    valid = (key_pos[None, :] <= query_pos[:, None]) & (key_pos[None, :] >= doc_begin[:, None])
    scores = jnp.where(valid[None, None], scores, masked_score)
    row_max = jnp.max(scores, axis=3, keepdims=True)
    exponent = jnp.exp(scores - row_max)
    probs = exponent / jnp.sum(exponent, axis=3, keepdims=True)
    dprob = jnp.einsum("tkgd,lkd->kgtl", upstream, values_all, preferred_element_type=jnp.float32)
    row_dot = jnp.sum(probs * dprob, axis=3, keepdims=True)
    probs_b = probs.astype(jnp.bfloat16)
    dscore = (probs * (dprob - row_dot)).astype(jnp.bfloat16)
    query_part = (
        jnp.einsum("kgtl,lkd->tkgd", dscore, keys_all, preferred_element_type=jnp.float32)
        * score_scale
    )
    key_part = (
        jnp.einsum("kgtl,tkgd->lkd", dscore, queries, preferred_element_type=jnp.float32)
        * score_scale
    )
    value_part = jnp.einsum("kgtl,tkgd->lkd", probs_b, upstream, preferred_element_type=jnp.float32)
    return (query_part, key_part, value_part)


def per_device(
    out_grad,
    expert_ids,
    top_logits,
    doc_start,
    router,
    w_down,
    saved_gu,
    out_weight,
    query,
    key,
    value,
):
    seq_count = lax.axis_size("seq")
    seq_index = lax.axis_index("seq")
    tokens_here = out_grad.shape[0]
    features = out_grad.shape[1]
    slots_all = saved_gu.shape[3]
    capacity = slots_all // seq_count
    experts = router.shape[0]
    top_count = expert_ids.shape[1]
    weights = jax.nn.softmax(top_logits, axis=1)
    hits = (expert_ids[:, :, None] == jnp.arange(experts, dtype=jnp.int32)[None, None, :]).astype(
        jnp.float32
    )
    per_token = jnp.sum(hits, axis=1)
    earlier = (jnp.arange(tokens_here)[:, None] > jnp.arange(tokens_here)[None, :]).astype(
        jnp.float32
    )
    before = jnp.dot(earlier, per_token, precision=highest)
    rank = jnp.sum(hits * before[:, None, :], axis=2).astype(jnp.int32)
    target = expert_ids * capacity + rank
    pad = -(-(capacity + 1) // 16) * 16
    padded_target = (expert_ids * pad + rank).reshape(-1)
    onehot = padded_target[None, :] == jnp.arange(experts * pad, dtype=jnp.int32)[:, None]
    token_of = (
        jnp.arange(tokens_here * top_count, dtype=jnp.int32)[:, None] // top_count
        == jnp.arange(tokens_here, dtype=jnp.int32)[None, :]
    ).astype(jnp.bfloat16)
    pick = jnp.dot(
        onehot.astype(jnp.bfloat16), token_of, preferred_element_type=jnp.float32
    ).astype(jnp.bfloat16)
    send_rows = jnp.dot(pick, out_grad, preferred_element_type=jnp.float32)
    send_weight = jnp.sum(jnp.where(onehot, weights.reshape(-1)[None, :], 0.0), axis=1)
    weight_row = jnp.pad(send_weight.reshape(experts, pad), ((0, 0), (0, features - pad)))
    is_weight = (jnp.arange(pad) == capacity)[None, :, None]
    payload = jnp.where(
        is_weight, weight_row[:, None, :], send_rows.reshape(experts, pad, features)
    ).astype(jnp.bfloat16)
    weight_full = lax.all_gather(out_weight, "seq", axis=1, tiled=True)
    kv_heads = key.shape[1]
    head_dim = key.shape[2]
    group = query.shape[1] // kv_heads
    paired = jnp.stack([key, value])
    blocks = [paired]
    for distance in range(1, REACH + 1):
        blocks.append(passed_along(paired, "seq", distance))
    payload, blocks = lax.optimization_barrier((payload, tuple(blocks)))
    sent_payload = lax.all_to_all(payload, "seq", split_axis=0, concat_axis=0, tiled=True)
    slot_rows = sent_payload[:, :capacity, :].reshape(slots_all, features)
    sent_weight = sent_payload[:, capacity, :capacity].reshape(slots_all)
    weight_here = w_down[0]
    head_count = lax.axis_size("head")
    partial = lax.dot_general(
        weight_here, slot_rows, (((1,), (1,)), ((), ())), preferred_element_type=jnp.float32
    ).astype(jnp.bfloat16)
    received = lax.all_to_all(
        partial.reshape(head_count, -1, slots_all), "head", split_axis=0, concat_axis=0, tiled=True
    )
    raw = jnp.sum(received.astype(jnp.float32), axis=0)
    gate = saved_gu[0, 0].astype(jnp.float32)
    up = saved_gu[0, 1].astype(jnp.float32)
    sig = jax.nn.sigmoid(gate)
    act = gate * sig
    hidden = act * up
    slot_part = jnp.sum(hidden * raw, axis=0)
    scaled = raw * sent_weight.reshape(slots_all).astype(jnp.float32)[None, :]
    gate_up_grad = jnp.stack([scaled * up * sig * (1.0 + gate * (1.0 - sig)), scaled * act])[
        None
    ].astype(jnp.bfloat16)
    slot_part, weight_full = lax.optimization_barrier((slot_part, weight_full))
    slot_grad = head_sum(slot_part)
    table = lax.all_gather(slot_grad, "seq", axis=0, tiled=True)
    lookup = expert_ids * slots_all + seq_index * capacity + rank
    route_grad = jnp.take(table, lookup.reshape(-1)).reshape(tokens_here, top_count)
    logit_grad = weights * (route_grad - jnp.sum(weights * route_grad, axis=1, keepdims=True))
    dense = jnp.einsum("tk,tke->te", logit_grad, hits, precision=highest)
    router_term = jnp.dot(dense, router.astype(jnp.float32), precision=highest)
    input_slice = (out_grad.astype(jnp.float32) + router_term).astype(jnp.bfloat16)
    input_grad = lax.all_gather(input_slice, "head", axis=1, tiled=True)
    attn_grad = lax.dot_general(
        input_grad,
        weight_full,
        (((1,), (1,)), ((), ())),
        preferred_element_type=jnp.float32,
    ).astype(jnp.bfloat16)
    window = jnp.concatenate(blocks[::-1], axis=1)
    local_pos = jnp.arange(tokens_here, dtype=jnp.int32)
    key_pos = jnp.concatenate(
        [(seq_index - distance) * tokens_here + local_pos for distance in range(REACH, -1, -1)]
    )
    query_pos = seq_index * tokens_here + local_pos
    queries = query.reshape(tokens_here, kv_heads, group, head_dim)
    upstream = attn_grad.reshape(tokens_here, kv_heads, group, head_dim)
    query_part, key_part, value_part = attend(
        queries, upstream, window[0], window[1], query_pos, key_pos, doc_start, head_dim ** (-0.5)
    )
    query_grad = query_part.reshape(query.shape).astype(jnp.bfloat16)
    pieces = jnp.stack([key_part, value_part]).reshape(
        2, REACH + 1, tokens_here, kv_heads, head_dim
    )
    totals = pieces[:, REACH]
    for distance in range(1, REACH + 1):
        totals = totals + passed_along(
            pieces[:, REACH - distance].astype(jnp.bfloat16), "seq", -distance
        ).astype(jnp.float32)
    return (
        gate_up_grad,
        route_grad,
        query_grad,
        totals[0].astype(jnp.bfloat16),
        totals[1].astype(jnp.bfloat16),
    )


def solution(mesh):
    in_specs = (
        P("seq", "head"),
        P("seq", None),
        P("seq", None),
        P("seq"),
        P(None, "head"),
        P("seq", None, "head"),
        P("seq", None, "head", None),
        P("head", "seq"),
        P("seq", "head", None),
        P("seq", "head", None),
        P("seq", "head", None),
    )
    out_specs = (
        P("seq", None, "head", None),
        P("seq", None),
        P("seq", "head", None),
        P("seq", "head", None),
        P("seq", "head", None),
    )
    return jax.shard_map(
        per_device, mesh=mesh, in_specs=in_specs, out_specs=out_specs, check_vma=False
    )
```

```python
import jax
import jax.numpy as jnp
from jax import lax
from jax.sharding import PartitionSpec as P

REACH = 7


masked_score = -1e30
highest = lax.Precision.HIGHEST


def passed_along(array, axis, by):
    count = lax.axis_size(axis)
    pairs = [(i, i + by) for i in range(count) if 0 <= i + by < count]
    return lax.ppermute(array, axis, pairs)


def head_sum(part):
    count = lax.axis_size("head")
    step = 1
    while step < count:
        pairs = [(i, i ^ step) for i in range(count)]
        part = part + lax.ppermute(part, "head", pairs)
        step *= 2
    return part


def attend(queries, upstream, keys_all, values_all, query_pos, key_pos, doc_begin, score_scale):
    scores = (
        jnp.einsum("tkgd,lkd->kgtl", queries, keys_all, preferred_element_type=jnp.float32)
        * score_scale
    )
    valid = (key_pos[None, :] <= query_pos[:, None]) & (key_pos[None, :] >= doc_begin[:, None])
    scores = jnp.where(valid[None, None], scores, masked_score)
    row_max = jnp.max(scores, axis=3, keepdims=True)
    exponent = jnp.exp(scores - row_max)
    probs = exponent / jnp.sum(exponent, axis=3, keepdims=True)
    dprob = jnp.einsum("tkgd,lkd->kgtl", upstream, values_all, preferred_element_type=jnp.float32)
    row_dot = jnp.sum(probs * dprob, axis=3, keepdims=True)
    probs_b = probs.astype(jnp.bfloat16)
    dscore = (probs * (dprob - row_dot)).astype(jnp.bfloat16)
    query_part = (
        jnp.einsum("kgtl,lkd->tkgd", dscore, keys_all, preferred_element_type=jnp.float32)
        * score_scale
    )
    key_part = (
        jnp.einsum("kgtl,tkgd->lkd", dscore, queries, preferred_element_type=jnp.float32)
        * score_scale
    )
    value_part = jnp.einsum("kgtl,tkgd->lkd", probs_b, upstream, preferred_element_type=jnp.float32)
    return (query_part, key_part, value_part)


def per_device(
    out_grad,
    expert_ids,
    top_logits,
    doc_start,
    router,
    w_down,
    saved_gu,
    out_weight,
    query,
    key,
    value,
):
    seq_count = lax.axis_size("seq")
    seq_index = lax.axis_index("seq")
    tokens_here = out_grad.shape[0]
    features = out_grad.shape[1]
    slots_all = saved_gu.shape[3]
    capacity = slots_all // seq_count
    experts = router.shape[0]
    top_count = expert_ids.shape[1]
    weights = jax.nn.softmax(top_logits, axis=1)
    hits = (expert_ids[:, :, None] == jnp.arange(experts, dtype=jnp.int32)[None, None, :]).astype(
        jnp.float32
    )
    per_token = jnp.sum(hits, axis=1)
    earlier = (jnp.arange(tokens_here)[:, None] > jnp.arange(tokens_here)[None, :]).astype(
        jnp.float32
    )
    before = jnp.dot(earlier, per_token, precision=highest)
    rank = jnp.sum(hits * before[:, None, :], axis=2).astype(jnp.int32)
    target = expert_ids * capacity + rank
    pad = -(-(capacity + 1) // 16) * 16
    padded_target = (expert_ids * pad + rank).reshape(-1)
    onehot = padded_target[None, :] == jnp.arange(experts * pad, dtype=jnp.int32)[:, None]
    token_of = (
        jnp.arange(tokens_here * top_count, dtype=jnp.int32)[:, None] // top_count
        == jnp.arange(tokens_here, dtype=jnp.int32)[None, :]
    ).astype(jnp.bfloat16)
    pick = jnp.dot(
        onehot.astype(jnp.bfloat16), token_of, preferred_element_type=jnp.float32
    ).astype(jnp.bfloat16)
    send_rows = jnp.dot(pick, out_grad, preferred_element_type=jnp.float32)
    send_weight = jnp.sum(jnp.where(onehot, weights.reshape(-1)[None, :], 0.0), axis=1)
    weight_row = jnp.pad(send_weight.reshape(experts, pad), ((0, 0), (0, features - pad)))
    is_weight = (jnp.arange(pad) == capacity)[None, :, None]
    payload = jnp.where(
        is_weight, weight_row[:, None, :], send_rows.reshape(experts, pad, features)
    ).astype(jnp.bfloat16)
    kv_heads = key.shape[1]
    head_dim = key.shape[2]
    group = query.shape[1] // kv_heads
    paired = jnp.stack([key, value])
    blocks = [paired]
    for distance in range(1, REACH + 1):
        blocks.append(passed_along(paired, "seq", distance))
    sent_payload = lax.all_to_all(payload, "seq", split_axis=0, concat_axis=0, tiled=True)
    sent_payload, blocks, weight_local = lax.optimization_barrier(
        (sent_payload, tuple(blocks), out_weight)
    )
    weight_full = lax.all_gather(weight_local, "seq", axis=1, tiled=True)
    slot_rows = sent_payload[:, :capacity, :].reshape(slots_all, features)
    sent_weight = sent_payload[:, capacity, :capacity].reshape(slots_all)
    weight_here = w_down[0]
    head_count = lax.axis_size("head")
    partial = lax.dot_general(
        weight_here, slot_rows, (((1,), (1,)), ((), ())), preferred_element_type=jnp.float32
    ).astype(jnp.bfloat16)
    received = lax.all_to_all(
        partial.reshape(head_count, -1, slots_all), "head", split_axis=0, concat_axis=0, tiled=True
    )
    raw = jnp.sum(received.astype(jnp.float32), axis=0)
    gate = saved_gu[0, 0].astype(jnp.float32)
    up = saved_gu[0, 1].astype(jnp.float32)
    sig = jax.nn.sigmoid(gate)
    act = gate * sig
    hidden = act * up
    slot_part = jnp.sum(hidden * raw, axis=0)
    scaled = raw * sent_weight.reshape(slots_all).astype(jnp.float32)[None, :]
    gate_up_grad = jnp.stack([scaled * up * sig * (1.0 + gate * (1.0 - sig)), scaled * act])[
        None
    ].astype(jnp.bfloat16)
    slot_grad = head_sum(slot_part)
    returned = lax.all_to_all(
        slot_grad.reshape(seq_count, capacity), "seq", split_axis=0, concat_axis=0, tiled=True
    )
    route_grad = jnp.take(returned.reshape(-1), target.reshape(-1)).reshape(tokens_here, top_count)
    logit_grad = weights * (route_grad - jnp.sum(weights * route_grad, axis=1, keepdims=True))
    dense = jnp.einsum("tk,tke->te", logit_grad, hits, precision=highest)
    router_term = jnp.dot(dense, router.astype(jnp.float32), precision=highest)
    input_slice = (out_grad.astype(jnp.float32) + router_term).astype(jnp.bfloat16)
    input_slice, weight_full = lax.optimization_barrier((input_slice, weight_full))
    input_grad = lax.all_gather(input_slice, "head", axis=1, tiled=True)
    attn_grad = lax.dot_general(
        input_grad,
        weight_full,
        (((1,), (1,)), ((), ())),
        preferred_element_type=jnp.float32,
    ).astype(jnp.bfloat16)
    window = jnp.concatenate(blocks[::-1], axis=1)
    local_pos = jnp.arange(tokens_here, dtype=jnp.int32)
    key_pos = jnp.concatenate(
        [(seq_index - distance) * tokens_here + local_pos for distance in range(REACH, -1, -1)]
    )
    query_pos = seq_index * tokens_here + local_pos
    queries = query.reshape(tokens_here, kv_heads, group, head_dim)
    upstream = attn_grad.reshape(tokens_here, kv_heads, group, head_dim)
    query_part, key_part, value_part = attend(
        queries, upstream, window[0], window[1], query_pos, key_pos, doc_start, head_dim ** (-0.5)
    )
    query_grad = query_part.reshape(query.shape).astype(jnp.bfloat16)
    pieces = jnp.stack([key_part, value_part]).reshape(
        2, REACH + 1, tokens_here, kv_heads, head_dim
    )
    current = pieces[:, ::-1]
    width = REACH + 1
    while width > 1:
        half = width // 2
        current = current[:, :half] + passed_along(
            current[:, half:width].astype(jnp.bfloat16), "seq", -half
        ).astype(jnp.float32)
        width = half
    totals = current[:, 0]
    return (
        gate_up_grad,
        route_grad,
        query_grad,
        totals[0].astype(jnp.bfloat16),
        totals[1].astype(jnp.bfloat16),
    )


def solution(mesh):
    in_specs = (
        P("seq", "head"),
        P("seq", None),
        P("seq", None),
        P("seq"),
        P(None, "head"),
        P("seq", None, "head"),
        P("seq", None, "head", None),
        P("head", "seq"),
        P("seq", "head", None),
        P("seq", "head", None),
        P("seq", "head", None),
    )
    out_specs = (
        P("seq", None, "head", None),
        P("seq", None),
        P("seq", "head", None),
        P("seq", "head", None),
        P("seq", "head", None),
    )
    return jax.shard_map(
        per_device, mesh=mesh, in_specs=in_specs, out_specs=out_specs, check_vma=False
    )
```

```python
import jax
import jax.numpy as jnp
from jax import lax
from jax.sharding import PartitionSpec as P

REACH = 7


masked_score = -1e30
highest = lax.Precision.HIGHEST


def passed_along(array, axis, by):
    count = lax.axis_size(axis)
    pairs = [(i, i + by) for i in range(count) if 0 <= i + by < count]
    return lax.ppermute(array, axis, pairs)


def head_sum(part):
    count = lax.axis_size("head")
    step = 1
    while step < count:
        pairs = [(i, i ^ step) for i in range(count)]
        part = part + lax.ppermute(part, "head", pairs)
        step *= 2
    return part


def attend(queries, upstream, keys_all, values_all, query_pos, key_pos, doc_begin, score_scale):
    scores = (
        jnp.einsum("tkgd,lkd->kgtl", queries, keys_all, preferred_element_type=jnp.float32)
        * score_scale
    )
    valid = (key_pos[None, :] <= query_pos[:, None]) & (key_pos[None, :] >= doc_begin[:, None])
    scores = jnp.where(valid[None, None], scores, masked_score)
    row_max = jnp.max(scores, axis=3, keepdims=True)
    exponent = jnp.exp(scores - row_max)
    probs = exponent / jnp.sum(exponent, axis=3, keepdims=True)
    dprob = jnp.einsum("tkgd,lkd->kgtl", upstream, values_all, preferred_element_type=jnp.float32)
    row_dot = jnp.sum(probs * dprob, axis=3, keepdims=True)
    probs_b = probs.astype(jnp.bfloat16)
    dscore = (probs * (dprob - row_dot)).astype(jnp.bfloat16)
    query_part = (
        jnp.einsum("kgtl,lkd->tkgd", dscore, keys_all, preferred_element_type=jnp.float32)
        * score_scale
    )
    key_part = (
        jnp.einsum("kgtl,tkgd->lkd", dscore, queries, preferred_element_type=jnp.float32)
        * score_scale
    )
    value_part = jnp.einsum("kgtl,tkgd->lkd", probs_b, upstream, preferred_element_type=jnp.float32)
    return (query_part, key_part, value_part)


def per_device(
    out_grad,
    expert_ids,
    top_logits,
    doc_start,
    router,
    w_down,
    saved_gu,
    out_weight,
    query,
    key,
    value,
):
    seq_count = lax.axis_size("seq")
    seq_index = lax.axis_index("seq")
    tokens_here = out_grad.shape[0]
    features = out_grad.shape[1]
    slots_all = saved_gu.shape[3]
    capacity = slots_all // seq_count
    experts = router.shape[0]
    top_count = expert_ids.shape[1]
    weights = jax.nn.softmax(top_logits, axis=1)
    hits = (expert_ids[:, :, None] == jnp.arange(experts, dtype=jnp.int32)[None, None, :]).astype(
        jnp.float32
    )
    per_token = jnp.sum(hits, axis=1)
    earlier = (jnp.arange(tokens_here)[:, None] > jnp.arange(tokens_here)[None, :]).astype(
        jnp.float32
    )
    before = jnp.dot(earlier, per_token, precision=highest)
    rank = jnp.sum(hits * before[:, None, :], axis=2).astype(jnp.int32)
    target = expert_ids * capacity + rank
    flat_target = target.reshape(-1)
    onehot = flat_target[None, :] == jnp.arange(experts * capacity, dtype=jnp.int32)[:, None]
    token_of = (
        jnp.arange(tokens_here * top_count, dtype=jnp.int32)[:, None] // top_count
        == jnp.arange(tokens_here, dtype=jnp.int32)[None, :]
    ).astype(jnp.bfloat16)
    pick = jnp.dot(
        onehot.astype(jnp.bfloat16), token_of, preferred_element_type=jnp.float32
    ).astype(jnp.bfloat16)
    send_rows = jnp.dot(pick, out_grad, preferred_element_type=jnp.float32).astype(jnp.bfloat16)
    send_weight = jnp.sum(jnp.where(onehot, weights.reshape(-1)[None, :], 0.0), axis=1)
    lanes = 128
    data_rows = capacity * features // lanes
    weight_tile = jnp.zeros((experts, 16, lanes), jnp.float32)
    weight_tile = weight_tile.at[:, 0, :capacity].set(send_weight.reshape(experts, capacity))
    payload = jnp.concatenate(
        [send_rows.reshape(experts, data_rows, lanes), weight_tile.astype(jnp.bfloat16)], axis=1
    )
    weight_full = lax.all_gather(out_weight, "seq", axis=1, tiled=True)
    kv_heads = key.shape[1]
    head_dim = key.shape[2]
    group = query.shape[1] // kv_heads
    paired = jnp.stack([key, value])
    blocks = [paired]
    for distance in range(1, REACH + 1):
        blocks.append(passed_along(paired, "seq", distance))
    sent_payload = lax.all_to_all(payload, "seq", split_axis=0, concat_axis=0, tiled=True)
    sent_payload, blocks = lax.optimization_barrier((sent_payload, tuple(blocks)))
    slot_rows = sent_payload[:, :data_rows, :].reshape(slots_all, features)
    sent_weight = sent_payload[:, data_rows, :capacity].reshape(slots_all)
    weight_here = w_down[0]
    head_count = lax.axis_size("head")
    partial = lax.dot_general(
        weight_here, slot_rows, (((1,), (1,)), ((), ())), preferred_element_type=jnp.float32
    ).astype(jnp.bfloat16)
    received = lax.all_to_all(
        partial.reshape(head_count, -1, slots_all), "head", split_axis=0, concat_axis=0, tiled=True
    )
    raw = jnp.sum(received.astype(jnp.float32), axis=0)
    gate = saved_gu[0, 0].astype(jnp.float32)
    up = saved_gu[0, 1].astype(jnp.float32)
    sig = jax.nn.sigmoid(gate)
    act = gate * sig
    hidden = act * up
    slot_part = jnp.sum(hidden * raw, axis=0)
    scaled = raw * sent_weight.reshape(slots_all).astype(jnp.float32)[None, :]
    gate_up_grad = jnp.stack([scaled * up * sig * (1.0 + gate * (1.0 - sig)), scaled * act])[
        None
    ].astype(jnp.bfloat16)
    slot_part, weight_full = lax.optimization_barrier((slot_part, weight_full))
    slot_grad = head_sum(slot_part)
    returned = lax.all_to_all(
        slot_grad.reshape(seq_count, capacity), "seq", split_axis=0, concat_axis=0, tiled=True
    )
    route_grad = jnp.take(returned.reshape(-1), target.reshape(-1)).reshape(tokens_here, top_count)
    logit_grad = weights * (route_grad - jnp.sum(weights * route_grad, axis=1, keepdims=True))
    dense = jnp.einsum("tk,tke->te", logit_grad, hits, precision=highest)
    router_term = jnp.dot(dense, router.astype(jnp.float32), precision=highest)
    input_slice = (out_grad.astype(jnp.float32) + router_term).astype(jnp.bfloat16)
    input_grad = lax.all_gather(input_slice, "head", axis=1, tiled=True)
    attn_grad = lax.dot_general(
        input_grad,
        weight_full,
        (((1,), (1,)), ((), ())),
        preferred_element_type=jnp.float32,
    ).astype(jnp.bfloat16)
    window = jnp.concatenate(blocks[::-1], axis=1)
    local_pos = jnp.arange(tokens_here, dtype=jnp.int32)
    key_pos = jnp.concatenate(
        [(seq_index - distance) * tokens_here + local_pos for distance in range(REACH, -1, -1)]
    )
    query_pos = seq_index * tokens_here + local_pos
    queries = query.reshape(tokens_here, kv_heads, group, head_dim)
    upstream = attn_grad.reshape(tokens_here, kv_heads, group, head_dim)
    query_part, key_part, value_part = attend(
        queries, upstream, window[0], window[1], query_pos, key_pos, doc_start, head_dim ** (-0.5)
    )
    query_grad = query_part.reshape(query.shape).astype(jnp.bfloat16)
    pieces = jnp.stack([key_part, value_part]).reshape(
        2, REACH + 1, tokens_here, kv_heads, head_dim
    )
    totals = pieces[:, REACH]
    for distance in range(1, REACH + 1):
        totals = totals + passed_along(
            pieces[:, REACH - distance].astype(jnp.bfloat16), "seq", -distance
        ).astype(jnp.float32)
    return (
        gate_up_grad,
        route_grad,
        query_grad,
        totals[0].astype(jnp.bfloat16),
        totals[1].astype(jnp.bfloat16),
    )


def solution(mesh):
    in_specs = (
        P("seq", "head"),
        P("seq", None),
        P("seq", None),
        P("seq"),
        P(None, "head"),
        P("seq", None, "head"),
        P("seq", None, "head", None),
        P("head", "seq"),
        P("seq", "head", None),
        P("seq", "head", None),
        P("seq", "head", None),
    )
    out_specs = (
        P("seq", None, "head", None),
        P("seq", None),
        P("seq", "head", None),
        P("seq", "head", None),
        P("seq", "head", None),
    )
    return jax.shard_map(
        per_device, mesh=mesh, in_specs=in_specs, out_specs=out_specs, check_vma=False
    )
```

```python
import jax
import jax.numpy as jnp
from jax import lax
from jax.sharding import PartitionSpec as P

REACH = 7


masked_score = -1e30
highest = lax.Precision.HIGHEST


def passed_along(array, axis, by):
    count = lax.axis_size(axis)
    pairs = [(i, i + by) for i in range(count) if 0 <= i + by < count]
    return lax.ppermute(array, axis, pairs)


def head_sum(part):
    count = lax.axis_size("head")
    step = 1
    while step < count:
        pairs = [(i, i ^ step) for i in range(count)]
        part = part + lax.ppermute(part, "head", pairs)
        step *= 2
    return part


def attend(queries, upstream, keys_all, values_all, query_pos, key_pos, doc_begin, score_scale):
    scores = (
        jnp.einsum("tkgd,lkd->kgtl", queries, keys_all, preferred_element_type=jnp.float32)
        * score_scale
    )
    valid = (key_pos[None, :] <= query_pos[:, None]) & (key_pos[None, :] >= doc_begin[:, None])
    scores = jnp.where(valid[None, None], scores, masked_score)
    row_max = jnp.max(scores, axis=3, keepdims=True)
    exponent = jnp.exp(scores - row_max)
    probs = exponent / jnp.sum(exponent, axis=3, keepdims=True)
    dprob = jnp.einsum("tkgd,lkd->kgtl", upstream, values_all, preferred_element_type=jnp.float32)
    row_dot = jnp.sum(probs * dprob, axis=3, keepdims=True)
    probs_b = probs.astype(jnp.bfloat16)
    dscore = (probs * (dprob - row_dot)).astype(jnp.bfloat16)
    query_part = (
        jnp.einsum("kgtl,lkd->tkgd", dscore, keys_all, preferred_element_type=jnp.float32)
        * score_scale
    )
    key_part = (
        jnp.einsum("kgtl,tkgd->lkd", dscore, queries, preferred_element_type=jnp.float32)
        * score_scale
    )
    value_part = jnp.einsum("kgtl,tkgd->lkd", probs_b, upstream, preferred_element_type=jnp.float32)
    return (query_part, key_part, value_part)


def per_device(
    out_grad,
    expert_ids,
    top_logits,
    doc_start,
    router,
    w_down,
    saved_gu,
    out_weight,
    query,
    key,
    value,
):
    seq_count = lax.axis_size("seq")
    seq_index = lax.axis_index("seq")
    tokens_here = out_grad.shape[0]
    features = out_grad.shape[1]
    slots_all = saved_gu.shape[3]
    capacity = slots_all // seq_count
    experts = router.shape[0]
    top_count = expert_ids.shape[1]
    weights = jax.nn.softmax(top_logits, axis=1)
    hits = (expert_ids[:, :, None] == jnp.arange(experts, dtype=jnp.int32)[None, None, :]).astype(
        jnp.float32
    )
    per_token = jnp.sum(hits, axis=1)
    earlier = (jnp.arange(tokens_here)[:, None] > jnp.arange(tokens_here)[None, :]).astype(
        jnp.float32
    )
    before = jnp.dot(earlier, per_token, precision=highest)
    rank = jnp.sum(hits * before[:, None, :], axis=2).astype(jnp.int32)
    target = expert_ids * capacity + rank
    pad = -(-(capacity + 1) // 16) * 16
    padded_target = (expert_ids * pad + rank).reshape(-1)
    onehot = padded_target[None, :] == jnp.arange(experts * pad, dtype=jnp.int32)[:, None]
    token_of = (
        jnp.arange(tokens_here * top_count, dtype=jnp.int32)[:, None] // top_count
        == jnp.arange(tokens_here, dtype=jnp.int32)[None, :]
    ).astype(jnp.bfloat16)
    pick = jnp.dot(
        onehot.astype(jnp.bfloat16), token_of, preferred_element_type=jnp.float32
    ).astype(jnp.bfloat16)
    send_rows = jnp.dot(pick, out_grad, preferred_element_type=jnp.float32)
    send_weight = jnp.sum(jnp.where(onehot, weights.reshape(-1)[None, :], 0.0), axis=1)
    weight_row = jnp.pad(send_weight.reshape(experts, pad), ((0, 0), (0, features - pad)))
    is_weight = (jnp.arange(pad) == capacity)[None, :, None]
    payload = jnp.where(
        is_weight, weight_row[:, None, :], send_rows.reshape(experts, pad, features)
    ).astype(jnp.bfloat16)
    weight_full = lax.all_gather(out_weight, "seq", axis=1, tiled=True)
    kv_heads = key.shape[1]
    head_dim = key.shape[2]
    group = query.shape[1] // kv_heads
    paired = jnp.stack([key, value])
    blocks = [paired]
    for distance in range(1, REACH + 1):
        blocks.append(passed_along(paired, "seq", distance))
    sent_payload = lax.all_to_all(payload, "seq", split_axis=0, concat_axis=0, tiled=True)
    sent_payload, blocks = lax.optimization_barrier((sent_payload, tuple(blocks)))
    slot_rows = sent_payload[:, :capacity, :].reshape(slots_all, features)
    sent_weight = sent_payload[:, capacity, :capacity].reshape(slots_all)
    weight_here = w_down[0]
    head_count = lax.axis_size("head")
    partial = lax.dot_general(
        weight_here, slot_rows, (((1,), (1,)), ((), ())), preferred_element_type=jnp.float32
    ).astype(jnp.bfloat16)
    received = lax.all_to_all(
        partial.reshape(head_count, -1, slots_all), "head", split_axis=0, concat_axis=0, tiled=True
    )
    raw = jnp.sum(received.astype(jnp.float32), axis=0)
    gate = saved_gu[0, 0].astype(jnp.float32)
    up = saved_gu[0, 1].astype(jnp.float32)
    sig = jax.nn.sigmoid(gate)
    act = gate * sig
    hidden = act * up
    slot_part = jnp.sum(hidden * raw, axis=0)
    scaled = raw * sent_weight.reshape(slots_all).astype(jnp.float32)[None, :]
    gate_up_grad = jnp.stack([scaled * up * sig * (1.0 + gate * (1.0 - sig)), scaled * act])[
        None
    ].astype(jnp.bfloat16)
    slot_grad = head_sum(slot_part)
    returned = lax.all_to_all(
        slot_grad.reshape(seq_count, capacity), "seq", split_axis=0, concat_axis=0, tiled=True
    )
    route_grad = jnp.take(returned.reshape(-1), target.reshape(-1)).reshape(tokens_here, top_count)
    logit_grad = weights * (route_grad - jnp.sum(weights * route_grad, axis=1, keepdims=True))
    dense = jnp.einsum("tk,tke->te", logit_grad, hits, precision=highest)
    router_term = jnp.dot(dense, router.astype(jnp.float32), precision=highest)
    input_slice = (out_grad.astype(jnp.float32) + router_term).astype(jnp.bfloat16)
    input_slice, weight_full = lax.optimization_barrier((input_slice, weight_full))
    input_grad = lax.all_gather(input_slice, "head", axis=1, tiled=True)
    attn_grad = lax.dot_general(
        input_grad,
        weight_full,
        (((1,), (1,)), ((), ())),
        preferred_element_type=jnp.float32,
    ).astype(jnp.bfloat16)
    window = jnp.concatenate(blocks[::-1], axis=1)
    local_pos = jnp.arange(tokens_here, dtype=jnp.int32)
    key_pos = jnp.concatenate(
        [(seq_index - distance) * tokens_here + local_pos for distance in range(REACH, -1, -1)]
    )
    query_pos = seq_index * tokens_here + local_pos
    queries = query.reshape(tokens_here, kv_heads, group, head_dim)
    upstream = attn_grad.reshape(tokens_here, kv_heads, group, head_dim)
    query_part, key_part, value_part = attend(
        queries, upstream, window[0], window[1], query_pos, key_pos, doc_start, head_dim ** (-0.5)
    )
    query_grad = query_part.reshape(query.shape).astype(jnp.bfloat16)
    pieces = jnp.stack([key_part, value_part]).reshape(
        2, REACH + 1, tokens_here, kv_heads, head_dim
    )
    totals = pieces[:, REACH]
    for distance in range(1, REACH + 1):
        totals = totals + passed_along(
            pieces[:, REACH - distance].astype(jnp.bfloat16), "seq", -distance
        ).astype(jnp.float32)
    return (
        gate_up_grad,
        route_grad,
        query_grad,
        totals[0].astype(jnp.bfloat16),
        totals[1].astype(jnp.bfloat16),
    )


def solution(mesh):
    in_specs = (
        P("seq", "head"),
        P("seq", None),
        P("seq", None),
        P("seq"),
        P(None, "head"),
        P("seq", None, "head"),
        P("seq", None, "head", None),
        P("head", "seq"),
        P("seq", "head", None),
        P("seq", "head", None),
        P("seq", "head", None),
    )
    out_specs = (
        P("seq", None, "head", None),
        P("seq", None),
        P("seq", "head", None),
        P("seq", "head", None),
        P("seq", "head", None),
    )
    return jax.shard_map(
        per_device, mesh=mesh, in_specs=in_specs, out_specs=out_specs, check_vma=False
    )
```

```python
import jax
import jax.numpy as jnp
from jax import lax
from jax.sharding import PartitionSpec as P

REACH = 7


masked_score = -1e30
highest = lax.Precision.HIGHEST


def passed_along(array, axis, by):
    count = lax.axis_size(axis)
    pairs = [(i, i + by) for i in range(count) if 0 <= i + by < count]
    return lax.ppermute(array, axis, pairs)


def head_sum(part):
    count = lax.axis_size("head")
    step = 1
    while step < count:
        pairs = [(i, i ^ step) for i in range(count)]
        part = part + lax.ppermute(part, "head", pairs)
        step *= 2
    return part


def attend(queries, upstream, keys_all, values_all, query_pos, key_pos, doc_begin, score_scale):
    scores = (
        jnp.einsum("tkgd,lkd->kgtl", queries, keys_all, preferred_element_type=jnp.float32)
        * score_scale
    )
    valid = (key_pos[None, :] <= query_pos[:, None]) & (key_pos[None, :] >= doc_begin[:, None])
    scores = jnp.where(valid[None, None], scores, masked_score)
    row_max = jnp.max(scores, axis=3, keepdims=True)
    exponent = jnp.exp(scores - row_max)
    probs = exponent / jnp.sum(exponent, axis=3, keepdims=True)
    dprob = jnp.einsum("tkgd,lkd->kgtl", upstream, values_all, preferred_element_type=jnp.float32)
    row_dot = jnp.sum(probs * dprob, axis=3, keepdims=True)
    probs_b = probs.astype(jnp.bfloat16)
    dscore = (probs * (dprob - row_dot)).astype(jnp.bfloat16)
    query_part = (
        jnp.einsum("kgtl,lkd->tkgd", dscore, keys_all, preferred_element_type=jnp.float32)
        * score_scale
    )
    key_part = (
        jnp.einsum("kgtl,tkgd->lkd", dscore, queries, preferred_element_type=jnp.float32)
        * score_scale
    )
    value_part = jnp.einsum("kgtl,tkgd->lkd", probs_b, upstream, preferred_element_type=jnp.float32)
    return (query_part, key_part, value_part)


def per_device(
    out_grad,
    expert_ids,
    top_logits,
    doc_start,
    router,
    w_down,
    saved_gu,
    out_weight,
    query,
    key,
    value,
):
    seq_count = lax.axis_size("seq")
    seq_index = lax.axis_index("seq")
    tokens_here = out_grad.shape[0]
    features = out_grad.shape[1]
    slots_all = saved_gu.shape[3]
    capacity = slots_all // seq_count
    experts = router.shape[0]
    top_count = expert_ids.shape[1]
    weights = jax.nn.softmax(top_logits, axis=1)
    hits = (expert_ids[:, :, None] == jnp.arange(experts, dtype=jnp.int32)[None, None, :]).astype(
        jnp.float32
    )
    per_token = jnp.sum(hits, axis=1)
    earlier = (jnp.arange(tokens_here)[:, None] > jnp.arange(tokens_here)[None, :]).astype(
        jnp.float32
    )
    before = jnp.dot(earlier, per_token, precision=highest)
    rank = jnp.sum(hits * before[:, None, :], axis=2).astype(jnp.int32)
    target = expert_ids * capacity + rank
    pad = -(-(capacity + 1) // 16) * 16
    padded_target = (expert_ids * pad + rank).reshape(-1)
    onehot = padded_target[None, :] == jnp.arange(experts * pad, dtype=jnp.int32)[:, None]
    token_of = (
        jnp.arange(tokens_here * top_count, dtype=jnp.int32)[:, None] // top_count
        == jnp.arange(tokens_here, dtype=jnp.int32)[None, :]
    ).astype(jnp.bfloat16)
    pick = jnp.dot(
        onehot.astype(jnp.bfloat16), token_of, preferred_element_type=jnp.float32
    ).astype(jnp.bfloat16)
    send_rows = jnp.dot(pick, out_grad, preferred_element_type=jnp.float32)
    send_weight = jnp.sum(jnp.where(onehot, weights.reshape(-1)[None, :], 0.0), axis=1)
    weight_row = jnp.pad(send_weight.reshape(experts, pad), ((0, 0), (0, features - pad)))
    is_weight = (jnp.arange(pad) == capacity)[None, :, None]
    payload = jnp.where(
        is_weight, weight_row[:, None, :], send_rows.reshape(experts, pad, features)
    ).astype(jnp.bfloat16)
    weight_full = lax.all_gather(out_weight, "seq", axis=1, tiled=True)
    kv_heads = key.shape[1]
    head_dim = key.shape[2]
    group = query.shape[1] // kv_heads
    paired = jnp.stack([key, value])
    blocks = [paired]
    for distance in range(1, REACH + 1):
        blocks.append(passed_along(paired, "seq", distance))
    sent_payload = lax.all_to_all(payload, "seq", split_axis=0, concat_axis=0, tiled=True)
    sent_payload, blocks = lax.optimization_barrier((sent_payload, tuple(blocks)))
    slot_rows = sent_payload[:, :capacity, :].reshape(slots_all, features)
    sent_weight = sent_payload[:, capacity, :capacity].reshape(slots_all)
    weight_here = w_down[0]
    head_count = lax.axis_size("head")
    partial = lax.dot_general(
        weight_here, slot_rows, (((1,), (1,)), ((), ())), preferred_element_type=jnp.float32
    ).astype(jnp.bfloat16)
    received = lax.all_to_all(
        partial.reshape(head_count, -1, slots_all), "head", split_axis=0, concat_axis=0, tiled=True
    )
    raw = jnp.sum(received.astype(jnp.float32), axis=0)
    gate = saved_gu[0, 0].astype(jnp.float32)
    up = saved_gu[0, 1].astype(jnp.float32)
    sig = jax.nn.sigmoid(gate)
    act = gate * sig
    hidden = act * up
    slot_part = jnp.sum(hidden * raw, axis=0)
    scaled = raw * sent_weight.reshape(slots_all).astype(jnp.float32)[None, :]
    gate_up_grad = jnp.stack([scaled * up * sig * (1.0 + gate * (1.0 - sig)), scaled * act])[
        None
    ].astype(jnp.bfloat16)
    slot_grad = head_sum(slot_part)
    returned = lax.all_to_all(
        slot_grad.reshape(seq_count, capacity), "seq", split_axis=0, concat_axis=0, tiled=True
    )
    flat_returned = returned.reshape(-1)
    match = target.reshape(-1)[:, None] == jnp.arange(slots_all, dtype=jnp.int32)[None, :]
    route_grad = jnp.sum(jnp.where(match, flat_returned[None, :], 0.0), axis=1).reshape(
        tokens_here, top_count
    )
    logit_grad = weights * (route_grad - jnp.sum(weights * route_grad, axis=1, keepdims=True))
    dense = jnp.einsum("tk,tke->te", logit_grad, hits, precision=highest)
    router_term = jnp.dot(dense, router.astype(jnp.float32), precision=highest)
    input_slice = (out_grad.astype(jnp.float32) + router_term).astype(jnp.bfloat16)
    input_slice, weight_full = lax.optimization_barrier((input_slice, weight_full))
    input_grad = lax.all_gather(input_slice, "head", axis=1, tiled=True)
    attn_grad = lax.dot_general(
        input_grad,
        weight_full,
        (((1,), (1,)), ((), ())),
        preferred_element_type=jnp.float32,
    ).astype(jnp.bfloat16)
    window = jnp.concatenate(blocks[::-1], axis=1)
    local_pos = jnp.arange(tokens_here, dtype=jnp.int32)
    key_pos = jnp.concatenate(
        [(seq_index - distance) * tokens_here + local_pos for distance in range(REACH, -1, -1)]
    )
    query_pos = seq_index * tokens_here + local_pos
    queries = query.reshape(tokens_here, kv_heads, group, head_dim)
    upstream = attn_grad.reshape(tokens_here, kv_heads, group, head_dim)
    query_part, key_part, value_part = attend(
        queries, upstream, window[0], window[1], query_pos, key_pos, doc_start, head_dim ** (-0.5)
    )
    query_grad = query_part.reshape(query.shape).astype(jnp.bfloat16)
    pieces = jnp.stack([key_part, value_part]).reshape(
        2, REACH + 1, tokens_here, kv_heads, head_dim
    )
    totals = pieces[:, REACH]
    for distance in range(1, REACH + 1):
        totals = totals + passed_along(
            pieces[:, REACH - distance].astype(jnp.bfloat16), "seq", -distance
        ).astype(jnp.float32)
    return (
        gate_up_grad,
        route_grad,
        query_grad,
        totals[0].astype(jnp.bfloat16),
        totals[1].astype(jnp.bfloat16),
    )


def solution(mesh):
    in_specs = (
        P("seq", "head"),
        P("seq", None),
        P("seq", None),
        P("seq"),
        P(None, "head"),
        P("seq", None, "head"),
        P("seq", None, "head", None),
        P("head", "seq"),
        P("seq", "head", None),
        P("seq", "head", None),
        P("seq", "head", None),
    )
    out_specs = (
        P("seq", None, "head", None),
        P("seq", None),
        P("seq", "head", None),
        P("seq", "head", None),
        P("seq", "head", None),
    )
    return jax.shard_map(
        per_device, mesh=mesh, in_specs=in_specs, out_specs=out_specs, check_vma=False
    )
```

```python
import jax
import jax.numpy as jnp
from jax import lax
from jax.sharding import PartitionSpec as P

REACH = 7


masked_score = -1e30
highest = lax.Precision.HIGHEST


def passed_along(array, axis, by):
    count = lax.axis_size(axis)
    pairs = [(i, i + by) for i in range(count) if 0 <= i + by < count]
    return lax.ppermute(array, axis, pairs)


def head_sum(part):
    count = lax.axis_size("head")
    step = 1
    while step < count:
        pairs = [(i, i ^ step) for i in range(count)]
        part = part + lax.ppermute(part, "head", pairs)
        step *= 2
    return part


def attend(queries, upstream, keys_all, values_all, query_pos, key_pos, doc_begin, score_scale):
    scores = (
        jnp.einsum("tkgd,lkd->kgtl", queries, keys_all, preferred_element_type=jnp.float32)
        * score_scale
    )
    valid = (key_pos[None, :] <= query_pos[:, None]) & (key_pos[None, :] >= doc_begin[:, None])
    scores = jnp.where(valid[None, None], scores, masked_score)
    row_max = jnp.max(scores, axis=3, keepdims=True)
    exponent = jnp.exp(scores - row_max)
    probs = exponent / jnp.sum(exponent, axis=3, keepdims=True)
    dprob = jnp.einsum("tkgd,lkd->kgtl", upstream, values_all, preferred_element_type=jnp.float32)
    row_dot = jnp.sum(probs * dprob, axis=3, keepdims=True)
    probs_b = probs.astype(jnp.bfloat16)
    dscore = (probs * (dprob - row_dot)).astype(jnp.bfloat16)
    query_part = (
        jnp.einsum("kgtl,lkd->tkgd", dscore, keys_all, preferred_element_type=jnp.float32)
        * score_scale
    )
    key_part = (
        jnp.einsum("kgtl,tkgd->lkd", dscore, queries, preferred_element_type=jnp.float32)
        * score_scale
    )
    value_part = jnp.einsum("kgtl,tkgd->lkd", probs_b, upstream, preferred_element_type=jnp.float32)
    return (query_part, key_part, value_part)


def per_device(
    out_grad,
    expert_ids,
    top_logits,
    doc_start,
    router,
    w_down,
    saved_gu,
    out_weight,
    query,
    key,
    value,
):
    seq_count = lax.axis_size("seq")
    seq_index = lax.axis_index("seq")
    tokens_here = out_grad.shape[0]
    features = out_grad.shape[1]
    slots_all = saved_gu.shape[3]
    capacity = slots_all // seq_count
    experts = router.shape[0]
    top_count = expert_ids.shape[1]
    weights = jax.nn.softmax(top_logits, axis=1)
    hits = (expert_ids[:, :, None] == jnp.arange(experts, dtype=jnp.int32)[None, None, :]).astype(
        jnp.float32
    )
    per_token = jnp.sum(hits, axis=1)
    earlier = (jnp.arange(tokens_here)[:, None] > jnp.arange(tokens_here)[None, :]).astype(
        jnp.float32
    )
    before = jnp.dot(earlier, per_token, precision=highest)
    rank = jnp.sum(hits * before[:, None, :], axis=2).astype(jnp.int32)
    target = expert_ids * capacity + rank
    flat_target = target.reshape(-1)
    onehot = flat_target[None, :] == jnp.arange(experts * capacity, dtype=jnp.int32)[:, None]
    token_of = (
        jnp.arange(tokens_here * top_count, dtype=jnp.int32)[:, None] // top_count
        == jnp.arange(tokens_here, dtype=jnp.int32)[None, :]
    ).astype(jnp.bfloat16)
    pick = jnp.dot(
        onehot.astype(jnp.bfloat16), token_of, preferred_element_type=jnp.float32
    ).astype(jnp.bfloat16)
    send_rows = jnp.dot(pick, out_grad, preferred_element_type=jnp.float32).astype(jnp.bfloat16)
    send_weight = jnp.sum(jnp.where(onehot, weights.reshape(-1)[None, :], 0.0), axis=1)
    lanes = 128
    data_rows = capacity * features // lanes
    weight_tile = jnp.zeros((experts, 16, lanes), jnp.float32)
    weight_tile = weight_tile.at[:, 0, :capacity].set(send_weight.reshape(experts, capacity))
    payload = jnp.concatenate(
        [send_rows.reshape(experts, data_rows, lanes), weight_tile.astype(jnp.bfloat16)], axis=1
    )
    weight_full = lax.all_gather(out_weight, "seq", axis=1, tiled=True)
    kv_heads = key.shape[1]
    head_dim = key.shape[2]
    group = query.shape[1] // kv_heads
    paired = jnp.stack([key, value])
    blocks = [paired]
    for distance in range(1, REACH + 1):
        blocks.append(passed_along(paired, "seq", distance))
    sent_payload = lax.all_to_all(payload, "seq", split_axis=0, concat_axis=0, tiled=True)
    sent_payload, blocks = lax.optimization_barrier((sent_payload, tuple(blocks)))
    slot_rows = sent_payload[:, :data_rows, :].reshape(slots_all, features)
    sent_weight = sent_payload[:, data_rows, :capacity].reshape(slots_all)
    weight_here = w_down[0]
    head_count = lax.axis_size("head")
    partial = lax.dot_general(
        weight_here, slot_rows, (((1,), (1,)), ((), ())), preferred_element_type=jnp.float32
    ).astype(jnp.bfloat16)
    received = lax.all_to_all(
        partial.reshape(head_count, -1, slots_all), "head", split_axis=0, concat_axis=0, tiled=True
    )
    raw = jnp.sum(received.astype(jnp.float32), axis=0)
    gate = saved_gu[0, 0].astype(jnp.float32)
    up = saved_gu[0, 1].astype(jnp.float32)
    sig = jax.nn.sigmoid(gate)
    act = gate * sig
    hidden = act * up
    slot_part = jnp.sum(hidden * raw, axis=0)
    scaled = raw * sent_weight.reshape(slots_all).astype(jnp.float32)[None, :]
    gate_up_grad = jnp.stack([scaled * up * sig * (1.0 + gate * (1.0 - sig)), scaled * act])[
        None
    ].astype(jnp.bfloat16)
    slot_grad = head_sum(slot_part)
    returned = lax.all_to_all(
        slot_grad.reshape(seq_count, capacity), "seq", split_axis=0, concat_axis=0, tiled=True
    )
    route_grad = jnp.take(returned.reshape(-1), target.reshape(-1)).reshape(tokens_here, top_count)
    logit_grad = weights * (route_grad - jnp.sum(weights * route_grad, axis=1, keepdims=True))
    dense = jnp.einsum("tk,tke->te", logit_grad, hits, precision=highest)
    router_term = jnp.dot(dense, router.astype(jnp.float32), precision=highest)
    input_slice = (out_grad.astype(jnp.float32) + router_term).astype(jnp.bfloat16)
    input_slice, weight_full = lax.optimization_barrier((input_slice, weight_full))
    input_grad = lax.all_gather(input_slice, "head", axis=1, tiled=True)
    attn_grad = lax.dot_general(
        input_grad,
        weight_full,
        (((1,), (1,)), ((), ())),
        preferred_element_type=jnp.float32,
    ).astype(jnp.bfloat16)
    window = jnp.concatenate(blocks[::-1], axis=1)
    local_pos = jnp.arange(tokens_here, dtype=jnp.int32)
    key_pos = jnp.concatenate(
        [(seq_index - distance) * tokens_here + local_pos for distance in range(REACH, -1, -1)]
    )
    query_pos = seq_index * tokens_here + local_pos
    queries = query.reshape(tokens_here, kv_heads, group, head_dim)
    upstream = attn_grad.reshape(tokens_here, kv_heads, group, head_dim)
    query_part, key_part, value_part = attend(
        queries, upstream, window[0], window[1], query_pos, key_pos, doc_start, head_dim ** (-0.5)
    )
    query_grad = query_part.reshape(query.shape).astype(jnp.bfloat16)
    pieces = jnp.stack([key_part, value_part]).reshape(
        2, REACH + 1, tokens_here, kv_heads, head_dim
    )
    totals = pieces[:, REACH]
    for distance in range(1, REACH + 1):
        totals = totals + passed_along(
            pieces[:, REACH - distance].astype(jnp.bfloat16), "seq", -distance
        ).astype(jnp.float32)
    return (
        gate_up_grad,
        route_grad,
        query_grad,
        totals[0].astype(jnp.bfloat16),
        totals[1].astype(jnp.bfloat16),
    )


def solution(mesh):
    in_specs = (
        P("seq", "head"),
        P("seq", None),
        P("seq", None),
        P("seq"),
        P(None, "head"),
        P("seq", None, "head"),
        P("seq", None, "head", None),
        P("head", "seq"),
        P("seq", "head", None),
        P("seq", "head", None),
        P("seq", "head", None),
    )
    out_specs = (
        P("seq", None, "head", None),
        P("seq", None),
        P("seq", "head", None),
        P("seq", "head", None),
        P("seq", "head", None),
    )
    return jax.shard_map(
        per_device, mesh=mesh, in_specs=in_specs, out_specs=out_specs, check_vma=False
    )
```
